512 devices in a mesh: sta: 32 (over z, x), slab: 16 (over y, core).
Axes of the slice: x: 4, y: 8, z: 8, core: 2. Of those that a mesh axis runs over, the one named last changes fastest.
Arguments:
- green_fields: bfloat16 [2, 64, 256, 4096], P(None, 'sta', 'slab'), may hold values from -6 to 6
- pair_list: int32 [256, 2], replicated, may hold values from 0 to 63
- pair_values: float32 [2, 256], replicated, may hold values from -6 to 6
- noise_map: float32 [256, 4096], P('slab'), may hold values from 0.1 to 1
- wave_square: float32 [256, 4096], P('slab'), may hold values from 0.1 to 1.5
- station_cell: int32 [64], P('sta'), may hold values from 0 to 1048575
Outputs:
- adjoint_field: float32 [2, 64, 256, 4096], P(None, 'sta', 'slab')
The draws below stay inside these ranges and needn't reach their ends.
Inputs may be any that keep to these rules, and one draw needn't show every extreme that they name: `pair_list`: pairs may repeat and may name one station twice; repeated entries add up. `station_cell`: index = depth layer * 64 * 64 + lateral index; stations may share a cell.
All inputs are finite; a program needn't handle non-finite values.
Results may differ from the reference program's by a relative error of at most 0.004.
Values may be sent and summed in bfloat16 or wider, within the bound.
No kernel may reach another device: no remote copies, remote signals or barrier semaphores. Data moves between devices by JAX's collectives and lax.ppermute only.
A program may use at most 64 MiB of HBM per device.

```python
import math
import jax
import jax.numpy as jnp
from jax import lax

GX = 64
GY = 64
SWEEPS = 6
STATIONS = 64
NZ = 256
PAIRS = 256


def with_ends(entries, stream_key, least, top_value):
    longest = entries.shape.index(max(entries.shape))
    spots = []
    for shift in (0, 1):
        where = [jax.random.randint(jax.random.fold_in(stream_key, axis), (), 0, length) for axis, length in enumerate(entries.shape)]
        where[longest] = (where[longest] + shift) % entries.shape[longest]
        spots.append(tuple(where))
    return entries.at[spots[0]].set(least).at[spots[1]].set(top_value)


def block_levels(key, shape, shards, least, largest):
    def one(dim, blocks):
        draws = jax.random.uniform(jax.random.fold_in(jax.random.fold_in(key, 6), dim), (blocks,), jnp.float32, least / len(shards), largest / len(shards))
        return jnp.repeat(jnp.exp(draws), shape[dim] // blocks).reshape((-1,) + (1,) * (len(shape) - dim - 1))

    factor_of = one(*shards[0])
    for cut in shards[1:]:
        factor_of = factor_of * one(*cut)
    return factor_of


def normal_values(stream_key, extent, deviation, most, pieces=(), kind=jnp.bfloat16):
    level = block_levels(stream_key, extent, pieces, -0.22, 0.18) if pieces else 1.0
    drawn = jax.random.normal(stream_key, extent, jnp.float32) * deviation * level
    return jnp.minimum(jnp.maximum(drawn, -most), most).astype(kind)


def setup_inputs(seed: int = 0) -> dict:
    key_of = jax.random.split(jax.random.key(seed), 7)
    return {
        "green_fields": normal_values(key_of[0], (2, STATIONS, NZ, GX * GY), 1.0, 6.0, ((1, 32), (2, 16))),
        "pair_list": with_ends(jax.random.randint(key_of[1], (PAIRS, 2), 0, STATIONS), jax.random.fold_in(key_of[1], 1), 0, STATIONS - 1).astype(jnp.int32),
        "pair_values": normal_values(key_of[2], (2, PAIRS), 1.0, 6.0, (), jnp.float32),
        "noise_map": jnp.clip(jnp.exp(math.log(1.0) - 2.3025851 * jax.random.uniform(key_of[3], (NZ, GX * GY), jnp.float32) ** block_levels(key_of[3], (NZ, GX * GY), ((0, 16),), -0.2, 0.2)), 0.1, 1.0),
        "wave_square": jnp.clip(jnp.exp(math.log(1.5) - 2.7080502 * jax.random.uniform(key_of[4], (NZ, GX * GY), jnp.float32) ** block_levels(key_of[4], (NZ, GX * GY), ((0, 16),), -0.2, 0.2)), 0.1, 1.5),
        "station_cell": with_ends(jax.random.randint(key_of[5], (STATIONS,), 0, NZ * GX * GY), jax.random.fold_in(key_of[5], 1), 0, (NZ * GX * GY) - 1).astype(jnp.int32),
    }


damping = 0.3
relaxation = 0.8
point_size = 2.0


def build_resid(pair_list, pair_values, count):
    labels = jnp.arange(count, dtype=jnp.int32)
    first = (pair_list[:, 0:1] == labels[None, :]).astype(jnp.float32)
    second = (pair_list[:, 1:2] == labels[None, :]).astype(jnp.float32)
    real_w = pair_values[0][:, None]
    imag_w = pair_values[1][:, None]
    highest = lax.Precision.HIGHEST
    resid_real = jnp.dot(first.T, real_w * second, precision=highest, preferred_element_type=jnp.float32) + jnp.dot(second.T, real_w * first, precision=highest, preferred_element_type=jnp.float32)
    resid_imag = jnp.dot(first.T, imag_w * second, precision=highest, preferred_element_type=jnp.float32) - jnp.dot(second.T, imag_w * first, precision=highest, preferred_element_type=jnp.float32)
    resid_real = resid_real.astype(jnp.bfloat16)
    resid_imag = resid_imag.astype(jnp.bfloat16)
    upper = jnp.concatenate([resid_real, -resid_imag], axis=1)
    lower = jnp.concatenate([resid_imag, resid_real], axis=1)
    return jnp.concatenate([upper, lower], axis=0)


def lateral(field, width_y):
    width = field.shape[-1]
    zeros_pad = [(0, 0)] * (field.ndim - 1)
    padded = jnp.pad(field, zeros_pad + [(width_y, width_y)])
    along_x = padded[..., :width] + padded[..., 2 * width_y:]
    column = jnp.arange(width, dtype=jnp.int32) % width_y
    stepped = jnp.pad(field, zeros_pad + [(1, 1)])
    left = stepped[..., :width] * (column != 0).astype(jnp.float32)
    right = stepped[..., 2:] * (column != width_y - 1).astype(jnp.float32)
    return along_x + left + right


def scales_from(wave):
    diag_real = 6.0 - wave
    denom = diag_real * diag_real + (damping * wave) * (damping * wave)
    return relaxation * diag_real / denom, relaxation * damping * wave / denom


def relax(padded, source, wave, scale_real, scale_imag, width_y):
    inner = padded[:, :, 1:-1]
    near = lateral(inner, width_y) + padded[:, :, :-2] + padded[:, :, 2:]
    real_in = inner[0]
    imag_in = inner[1]
    applied_real = 6.0 * real_in - near[0] - wave * (real_in - damping * imag_in)
    applied_imag = 6.0 * imag_in - near[1] - wave * (damping * real_in + imag_in)
    rest_real = source[0] - applied_real
    rest_imag = source[1] - applied_imag
    return jnp.stack([real_in + scale_real * rest_real - scale_imag * rest_imag, imag_in + scale_real * rest_imag + scale_imag * rest_real])


def reference(green_fields, pair_list, pair_values, noise_map, wave_square, station_cell):
    count = green_fields.shape[1]
    depth = green_fields.shape[2]
    cells = green_fields.shape[3]
    big = build_resid(pair_list, pair_values, count)
    flat = green_fields.reshape(2 * count, depth * cells)
    adjoint = jnp.dot(big, flat, preferred_element_type=jnp.float32).astype(jnp.bfloat16)
    adjoint = adjoint.reshape(2, count, depth, cells)
    scale_real, scale_imag = scales_from(wave_square)
    flat_cells = jnp.arange(depth * cells, dtype=jnp.int32)

    def one_station(index):
        part = lax.dynamic_index_in_dim(adjoint, index, 1, keepdims=True).astype(jnp.float32)
        spot = (flat_cells == station_cell[index]).astype(jnp.float32).reshape(1, depth, cells) * point_size
        source = noise_map[None, None] * part
        source = jnp.stack([source[0] + spot, source[1]])
        field = jnp.zeros((2, 1, depth, cells), jnp.float32)
        for repeat in range(SWEEPS):
            padded = jnp.pad(field, ((0, 0), (0, 0), (1, 1), (0, 0)))
            field = relax(padded, source, wave_square, scale_real, scale_imag, GY)
        return field[:, 0]

    result = lax.map(one_station, jnp.arange(count, dtype=jnp.int32))
    return jnp.transpose(result, (1, 0, 2, 3))
```

```python
import functools

import jax
import jax.numpy as jnp
from jax import lax
from jax.experimental import pallas as pl
from jax.experimental.pallas import tpu as pltpu
from jax.sharding import PartitionSpec as P

GY = 64
SWEEPS = 6
HALO = 8

damping = 0.3
relaxation = 0.8
point_size = 2.0


def build_resid(pair_list, pair_values, count):
    labels = jnp.arange(count, dtype=jnp.int32)
    first = (pair_list[:, 0:1] == labels[None, :]).astype(jnp.float32)
    second = (pair_list[:, 1:2] == labels[None, :]).astype(jnp.float32)
    real_w = pair_values[0][:, None]
    imag_w = pair_values[1][:, None]
    highest = lax.Precision.HIGHEST
    resid_real = jnp.dot(
        first.T, real_w * second, precision=highest, preferred_element_type=jnp.float32
    ) + jnp.dot(second.T, real_w * first, precision=highest, preferred_element_type=jnp.float32)
    resid_imag = jnp.dot(
        first.T, imag_w * second, precision=highest, preferred_element_type=jnp.float32
    ) - jnp.dot(second.T, imag_w * first, precision=highest, preferred_element_type=jnp.float32)
    resid_real = resid_real.astype(jnp.bfloat16)
    resid_imag = resid_imag.astype(jnp.bfloat16)
    upper = jnp.concatenate([resid_real, -resid_imag], axis=1)
    lower = jnp.concatenate([resid_imag, resid_real], axis=1)
    return jnp.concatenate([upper, lower], axis=0)


def mix_kernel(depth, big_ref, recv_ref, out_ref, wide_ref, acc_ref):
    wide_ref[...] = recv_ref[...].astype(jnp.float32)
    big = big_ref[...]
    rows = big.shape[0]
    for r in range(depth):
        rhs = wide_ref[pl.ds(r, rows, stride=depth), :].astype(jnp.bfloat16)
        acc_ref[pl.ds(r, rows, stride=depth), :] = jnp.dot(
            big, rhs, preferred_element_type=jnp.float32
        )
    out_ref[...] = acc_ref[...].astype(out_ref.dtype)


def mix(big, recv, depth):
    total, lanes = recv.shape
    return pl.pallas_call(
        functools.partial(mix_kernel, depth),
        out_shape=jax.ShapeDtypeStruct((total, lanes), jnp.bfloat16),
        scratch_shapes=[
            pltpu.VMEM((total, lanes), jnp.float32),
            pltpu.VMEM((total, lanes), jnp.float32),
        ],
        cost_estimate=pl.CostEstimate(
            flops=2 * big.shape[0] * big.shape[1] * depth * lanes,
            bytes_accessed=4 * total * lanes,
            transcendentals=0,
        ),
    )(big, recv)


def source_kernel(owned, depth, meta_ref, recv_ref, noise_ref, lo_ref, hi_ref):
    pieces, _, lanes = recv_ref.shape
    half = depth // 2
    slab = meta_ref[0]
    row = lax.broadcasted_iota(jnp.int32, (depth, lanes), 0)
    lane = lax.broadcasted_iota(jnp.int32, (depth, lanes), 1)
    base = (slab * depth + row) * (pieces * lanes) + lane
    for b in range(owned):
        spot_at = meta_ref[2 + b]
        for part in range(2):
            start = (b * 2 + part) * depth
            for ct in range(pieces):
                cols = slice(ct * lanes, (ct + 1) * lanes)
                tile = recv_ref[ct, start : start + depth, :].astype(jnp.float32)
                value = noise_ref[:, cols] * tile
                if part == 0:
                    hit = base + ct * lanes == spot_at
                    value = value + jnp.where(hit, point_size, 0.0)
                lo_ref[b, part, :, cols] = value[:half]
                hi_ref[b, part, :, cols] = value[half:]


def sweep_kernel(depth, meta_ref, lo_ref, hi_ref, below_ref, above_ref, wave_ref, wbelow_ref,
                 wabove_ref, out_ref, re_ref, im_ref, sre_ref, sim_ref, w_ref, sr_ref, si_ref):
    half = depth // 2
    rows, cells = re_ref.shape
    slab = meta_ref[0]
    nslab = meta_ref[1]
    w_ref[0:HALO] = wbelow_ref[...]
    w_ref[HALO : HALO + depth] = wave_ref[...]
    w_ref[HALO + depth :] = wabove_ref[...]
    for part, dst in ((0, sre_ref), (1, sim_ref)):
        dst[0:HALO] = below_ref[0, part]
        dst[HALO : HALO + half] = lo_ref[0, part]
        dst[HALO + half : HALO + depth] = hi_ref[0, part]
        dst[HALO + depth :] = above_ref[0, part]
    wave = w_ref[...]
    row = lax.broadcasted_iota(jnp.int32, (rows, cells), 0)
    inside = jnp.logical_and(
        jnp.logical_or(row >= HALO, slab > 0),
        jnp.logical_or(row < HALO + depth, slab < nslab - 1),
    )
    diag_real = 6.0 - wave
    denom = diag_real * diag_real + damping * wave * (damping * wave)
    sr_ref[...] = jnp.where(inside, relaxation * diag_real / denom, 0.0)
    si_ref[...] = jnp.where(inside, relaxation * damping * wave / denom, 0.0)
    sr = sr_ref[...]
    si = si_ref[...]
    src_re = sre_ref[...]
    src_im = sim_ref[...]
    re_ref[...] = sr * src_re - si * src_im
    im_ref[...] = sr * src_im + si * src_re

    def near(f, lane):
        col = lane % GY
        xm = jnp.where(lane >= GY, pltpu.roll(f, GY, 1), 0.0)
        xp = jnp.where(lane < cells - GY, pltpu.roll(f, cells - GY, 1), 0.0)
        ym = jnp.where(col != 0, pltpu.roll(f, 1, 1), 0.0)
        yp = jnp.where(col != GY - 1, pltpu.roll(f, cells - 1, 1), 0.0)
        dn = pltpu.roll(f, 1, 0)
        up = pltpu.roll(f, rows - 1, 0)
        return xm + xp + ym + yp + dn + up

    def body(_, carry):
        lane = lax.broadcasted_iota(jnp.int32, (rows, cells), 1)
        re = re_ref[...]
        im = im_ref[...]
        w = w_ref[...]
        near_re = near(re, lane)
        near_im = near(im, lane)
        applied_re = 6.0 * re - near_re - w * (re - damping * im)
        applied_im = 6.0 * im - near_im - w * (damping * re + im)
        rest_re = sre_ref[...] - applied_re
        rest_im = sim_ref[...] - applied_im
        s_r = sr_ref[...]
        s_i = si_ref[...]
        re_ref[...] = re + s_r * rest_re - s_i * rest_im
        im_ref[...] = im + s_r * rest_im + s_i * rest_re
        return carry

    lax.fori_loop(0, SWEEPS - 1, body, 0)
    out_ref[0, 0] = re_ref[HALO : HALO + depth]
    out_ref[1, 0] = im_ref[HALO : HALO + depth]


def sweeps(meta, lo, hi, below, above, wave, wbelow, wabove):
    owned, _, half, cells = lo.shape
    depth = 2 * half
    rows = depth + 2 * HALO
    piece = pl.BlockSpec((1, 2, half, cells), lambda b, *_: (b, 0, 0, 0))
    halo = pl.BlockSpec((1, 2, HALO, cells), lambda b, *_: (b, 0, 0, 0))
    whole = lambda shape: pl.BlockSpec(shape, lambda b, *_: (0,) * len(shape))
    grid_spec = pltpu.PrefetchScalarGridSpec(
        num_scalar_prefetch=1,
        grid=(owned,),
        in_specs=[piece, piece, halo, halo, whole((depth, cells)), whole((HALO, cells)),
                  whole((HALO, cells))],
        out_specs=pl.BlockSpec((2, 1, depth, cells), lambda b, *_: (0, b, 0, 0)),
        scratch_shapes=[pltpu.VMEM((rows, cells), jnp.float32) for _ in range(7)],
    )
    return pl.pallas_call(
        functools.partial(sweep_kernel, depth),
        out_shape=jax.ShapeDtypeStruct((2, owned, depth, cells), jnp.float32),
        grid_spec=grid_spec,
        cost_estimate=pl.CostEstimate(
            flops=owned * SWEEPS * 90 * rows * cells,
            bytes_accessed=owned * 4 * cells * (6 * depth),
            transcendentals=0,
        ),
    )(meta, lo, hi, below, above, wave, wbelow, wabove)


def local(green_fields, pair_list, pair_values, noise_map, wave_square, station_cell):
    parts, owned, depth, cells = green_fields.shape
    nsta = lax.axis_size("sta")
    nslab = lax.axis_size("slab")
    count = owned * nsta
    lanes = cells // nsta
    slab = lax.axis_index("slab")
    up_pairs = [(i, i + 1) for i in range(nslab - 1)]
    down_pairs = [(i + 1, i) for i in range(nslab - 1)]
    half = depth // 2

    wbelow = lax.ppermute(wave_square[depth - HALO :], "slab", up_pairs)
    wabove = lax.ppermute(wave_square[:HALO], "slab", down_pairs)

    send = green_fields.reshape(parts, owned, depth, nsta, lanes)
    send = send.transpose(3, 0, 1, 2, 4).reshape(nsta, parts * owned * depth, lanes)
    recv = lax.all_to_all(send, "sta", 0, 0, tiled=True)

    big = build_resid(pair_list, pair_values, count)
    big = big.reshape(2, count, 2, nsta, owned).transpose(1, 0, 3, 2, 4)
    big = big.reshape(2 * count, 2 * count)
    mixed = mix(big, recv.reshape(nsta * parts * owned * depth, lanes), depth)
    back = lax.all_to_all(mixed.reshape(nsta, owned * parts * depth, lanes), "sta", 0, 0,
                          tiled=True)

    meta = jnp.concatenate(
        [jnp.stack([slab, jnp.int32(nslab)]).astype(jnp.int32), station_cell.astype(jnp.int32)]
    )
    lo, hi = pl.pallas_call(
        functools.partial(source_kernel, owned, depth),
        out_shape=[jax.ShapeDtypeStruct((owned, 2, half, cells), jnp.float32)] * 2,
        in_specs=[
            pl.BlockSpec(memory_space=pltpu.SMEM),
            pl.BlockSpec(memory_space=pltpu.VMEM),
            pl.BlockSpec(memory_space=pltpu.VMEM),
        ],
    )(meta, back, noise_map)
    below = lax.ppermute(hi, "slab", up_pairs)
    above = lax.ppermute(lo, "slab", down_pairs)
    return sweeps(meta, lo, hi, below, above, wave_square, wbelow, wabove)


def solution(mesh):
    placed = (P(None, "sta", "slab", None), P(), P(), P("slab", None), P("slab", None), P("sta"))
    return jax.shard_map(
        local, mesh=mesh, in_specs=placed, out_specs=P(None, "sta", "slab", None), check_vma=False
    )
```

```python
import functools

import jax
import jax.numpy as jnp
from jax import lax
from jax.experimental import pallas as pl
from jax.experimental.pallas import tpu as pltpu
from jax.sharding import PartitionSpec as P

GY = 64
SWEEPS = 6
HALO = 8

damping = 0.3
relaxation = 0.8
point_size = 2.0


def build_resid(pair_list, pair_values, count):
    labels = jnp.arange(count, dtype=jnp.int32)
    first = (pair_list[:, 0:1] == labels[None, :]).astype(jnp.float32)
    second = (pair_list[:, 1:2] == labels[None, :]).astype(jnp.float32)
    real_w = pair_values[0][:, None]
    imag_w = pair_values[1][:, None]
    highest = lax.Precision.HIGHEST
    resid_real = jnp.dot(
        first.T, real_w * second, precision=highest, preferred_element_type=jnp.float32
    ) + jnp.dot(second.T, real_w * first, precision=highest, preferred_element_type=jnp.float32)
    resid_imag = jnp.dot(
        first.T, imag_w * second, precision=highest, preferred_element_type=jnp.float32
    ) - jnp.dot(second.T, imag_w * first, precision=highest, preferred_element_type=jnp.float32)
    resid_real = resid_real.astype(jnp.bfloat16)
    resid_imag = resid_imag.astype(jnp.bfloat16)
    upper = jnp.concatenate([resid_real, -resid_imag], axis=1)
    lower = jnp.concatenate([resid_imag, resid_real], axis=1)
    return jnp.concatenate([upper, lower], axis=0)


def mix_kernel(depth, big_ref, recv_ref, out_ref, wide_ref, acc_ref):
    wide_ref[...] = recv_ref[...].astype(jnp.float32)
    big = big_ref[...]
    rows = big.shape[0]
    for r in range(depth):
        rhs = wide_ref[pl.ds(r, rows, stride=depth), :].astype(jnp.bfloat16)
        acc_ref[pl.ds(r, rows, stride=depth), :] = jnp.dot(
            big, rhs, preferred_element_type=jnp.float32
        )
    out_ref[...] = acc_ref[...].astype(out_ref.dtype)


def mix(big, recv, depth):
    total, lanes = recv.shape
    return pl.pallas_call(
        functools.partial(mix_kernel, depth),
        out_shape=jax.ShapeDtypeStruct((total, lanes), jnp.bfloat16),
        scratch_shapes=[
            pltpu.VMEM((total, lanes), jnp.float32),
            pltpu.VMEM((total, lanes), jnp.float32),
        ],
        cost_estimate=pl.CostEstimate(
            flops=2 * big.shape[0] * big.shape[1] * depth * lanes,
            bytes_accessed=4 * total * lanes,
            transcendentals=0,
        ),
    )(big, recv)


def source_kernel(owned, depth, meta_ref, recv_ref, noise_ref, lo_ref, hi_ref):
    pieces, _, lanes = recv_ref.shape
    half = depth // 2
    slab = meta_ref[0]
    row = lax.broadcasted_iota(jnp.int32, (depth, lanes), 0)
    lane = lax.broadcasted_iota(jnp.int32, (depth, lanes), 1)
    base = (slab * depth + row) * (pieces * lanes) + lane
    for b in range(owned):
        spot_at = meta_ref[2 + b]
        for part in range(2):
            start = (b * 2 + part) * depth
            for ct in range(pieces):
                cols = slice(ct * lanes, (ct + 1) * lanes)
                tile = recv_ref[ct, start : start + depth, :].astype(jnp.float32)
                value = noise_ref[:, cols] * tile
                if part == 0:
                    hit = base + ct * lanes == spot_at
                    value = value + jnp.where(hit, point_size, 0.0)
                lo_ref[b, part, :, cols] = value[:half]
                hi_ref[b, part, :, cols] = value[half:]


def sweep_kernel(depth, meta_ref, lo_ref, hi_ref, below_ref, above_ref, wave_ref, wbelow_ref,
                 wabove_ref, out_ref, re_ref, im_ref, sre_ref, sim_ref, w_ref, sr_ref, si_ref):
    half = depth // 2
    rows, cells = re_ref.shape
    slab = meta_ref[0]
    nslab = meta_ref[1]
    w_ref[0:HALO] = wbelow_ref[...]
    w_ref[HALO : HALO + depth] = wave_ref[...]
    w_ref[HALO + depth :] = wabove_ref[...]
    for part, dst in ((0, sre_ref), (1, sim_ref)):
        dst[0:HALO] = below_ref[0, part]
        dst[HALO : HALO + half] = lo_ref[0, part]
        dst[HALO + half : HALO + depth] = hi_ref[0, part]
        dst[HALO + depth :] = above_ref[0, part]
    wave = w_ref[...]
    row = lax.broadcasted_iota(jnp.int32, (rows, cells), 0)
    inside = jnp.logical_and(
        jnp.logical_or(row >= HALO, slab > 0),
        jnp.logical_or(row < HALO + depth, slab < nslab - 1),
    )
    diag_real = 6.0 - wave
    denom = diag_real * diag_real + damping * wave * (damping * wave)
    sr_ref[...] = jnp.where(inside, relaxation * diag_real / denom, 0.0)
    si_ref[...] = jnp.where(inside, relaxation * damping * wave / denom, 0.0)
    sr = sr_ref[...]
    si = si_ref[...]
    src_re = sre_ref[...]
    src_im = sim_ref[...]
    re_ref[...] = sr * src_re - si * src_im
    im_ref[...] = sr * src_im + si * src_re

    keep = 1.0 - relaxation

    def body(_, carry):
        lane = lax.broadcasted_iota(jnp.int32, (rows, cells), 1)
        col = jnp.bitwise_and(lane, GY - 1)
        has_xm = lane >= GY
        has_xp = lane < cells - GY
        has_ym = col != 0
        has_yp = col != GY - 1

        def total(f, src):
            shifted = pltpu.roll(f, GY, 1)
            xm = jnp.where(has_xm, shifted, 0.0)
            xp = jnp.where(has_xp, pltpu.roll(shifted, cells - 2 * GY, 1), 0.0)
            ym = jnp.where(has_ym, pltpu.roll(f, 1, 1), 0.0)
            yp = jnp.where(has_yp, pltpu.roll(f, cells - 1, 1), 0.0)
            dn = pltpu.roll(f, 1, 0)
            up = pltpu.roll(f, rows - 1, 0)
            return src + (xm + xp + ym + yp + dn + up)

        re = re_ref[...]
        im = im_ref[...]
        t_re = total(re, sre_ref[...])
        t_im = total(im, sim_ref[...])
        s_r = sr_ref[...]
        s_i = si_ref[...]
        re_ref[...] = keep * re + (s_r * t_re - s_i * t_im)
        im_ref[...] = keep * im + (s_r * t_im + s_i * t_re)
        return carry

    lax.fori_loop(0, SWEEPS - 1, body, 0)
    out_ref[0, 0] = re_ref[HALO : HALO + depth]
    out_ref[1, 0] = im_ref[HALO : HALO + depth]


def sweeps(meta, lo, hi, below, above, wave, wbelow, wabove):
    owned, _, half, cells = lo.shape
    depth = 2 * half
    rows = depth + 2 * HALO
    piece = pl.BlockSpec((1, 2, half, cells), lambda b, *_: (b, 0, 0, 0))
    halo = pl.BlockSpec((1, 2, HALO, cells), lambda b, *_: (b, 0, 0, 0))
    whole = lambda shape: pl.BlockSpec(shape, lambda b, *_: (0,) * len(shape))
    grid_spec = pltpu.PrefetchScalarGridSpec(
        num_scalar_prefetch=1,
        grid=(owned,),
        in_specs=[piece, piece, halo, halo, whole((depth, cells)), whole((HALO, cells)),
                  whole((HALO, cells))],
        out_specs=pl.BlockSpec((2, 1, depth, cells), lambda b, *_: (0, b, 0, 0)),
        scratch_shapes=[pltpu.VMEM((rows, cells), jnp.float32) for _ in range(7)],
    )
    return pl.pallas_call(
        functools.partial(sweep_kernel, depth),
        out_shape=jax.ShapeDtypeStruct((2, owned, depth, cells), jnp.float32),
        grid_spec=grid_spec,
        cost_estimate=pl.CostEstimate(
            flops=owned * SWEEPS * 90 * rows * cells,
            bytes_accessed=owned * 4 * cells * (6 * depth),
            transcendentals=0,
        ),
    )(meta, lo, hi, below, above, wave, wbelow, wabove)


def local(green_fields, pair_list, pair_values, noise_map, wave_square, station_cell):
    parts, owned, depth, cells = green_fields.shape
    nsta = lax.axis_size("sta")
    nslab = lax.axis_size("slab")
    count = owned * nsta
    lanes = cells // nsta
    slab = lax.axis_index("slab")
    up_pairs = [(i, i + 1) for i in range(nslab - 1)]
    down_pairs = [(i + 1, i) for i in range(nslab - 1)]
    half = depth // 2

    wbelow = lax.ppermute(wave_square[depth - HALO :], "slab", up_pairs)
    wabove = lax.ppermute(wave_square[:HALO], "slab", down_pairs)

    send = green_fields.reshape(parts, owned, depth, nsta, lanes)
    send = send.transpose(3, 0, 1, 2, 4).reshape(nsta, parts * owned * depth, lanes)
    recv = lax.all_to_all(send, "sta", 0, 0, tiled=True)

    big = build_resid(pair_list, pair_values, count)
    big = big.reshape(2, count, 2, nsta, owned).transpose(1, 0, 3, 2, 4)
    big = big.reshape(2 * count, 2 * count)
    big, wbelow, wabove = lax.optimization_barrier((big, wbelow, wabove))
    mixed = mix(big, recv.reshape(nsta * parts * owned * depth, lanes), depth)
    back = lax.all_to_all(mixed.reshape(nsta, owned * parts * depth, lanes), "sta", 0, 0,
                          tiled=True)

    meta = jnp.concatenate(
        [jnp.stack([slab, jnp.int32(nslab)]).astype(jnp.int32), station_cell.astype(jnp.int32)]
    )
    lo, hi = pl.pallas_call(
        functools.partial(source_kernel, owned, depth),
        out_shape=[jax.ShapeDtypeStruct((owned, 2, half, cells), jnp.float32)] * 2,
        in_specs=[
            pl.BlockSpec(memory_space=pltpu.SMEM),
            pl.BlockSpec(memory_space=pltpu.VMEM),
            pl.BlockSpec(memory_space=pltpu.VMEM),
        ],
    )(meta, back, noise_map)
    below = lax.ppermute(hi, "slab", up_pairs)
    above = lax.ppermute(lo, "slab", down_pairs)
    return sweeps(meta, lo, hi, below, above, wave_square, wbelow, wabove)


def solution(mesh):
    placed = (P(None, "sta", "slab", None), P(), P(), P("slab", None), P("slab", None), P("sta"))
    return jax.shard_map(
        local, mesh=mesh, in_specs=placed, out_specs=P(None, "sta", "slab", None), check_vma=False
    )
```

```python
import functools

import jax
import jax.numpy as jnp
from jax import lax
from jax.experimental import pallas as pl
from jax.experimental.pallas import tpu as pltpu
from jax.sharding import PartitionSpec as P

GY = 64
SWEEPS = 6
HALO = 8
LANES = 128
PAD = 128

damping = 0.3
relaxation = 0.8
point_size = 2.0


def build_resid(pair_list, pair_values, count):
    labels = jnp.arange(count, dtype=jnp.int32)
    first = (pair_list[:, 0:1] == labels[None, :]).astype(jnp.float32)
    second = (pair_list[:, 1:2] == labels[None, :]).astype(jnp.float32)
    real_w = pair_values[0][:, None]
    imag_w = pair_values[1][:, None]
    highest = lax.Precision.HIGHEST
    resid_real = jnp.dot(
        first.T, real_w * second, precision=highest, preferred_element_type=jnp.float32
    ) + jnp.dot(second.T, real_w * first, precision=highest, preferred_element_type=jnp.float32)
    resid_imag = jnp.dot(
        first.T, imag_w * second, precision=highest, preferred_element_type=jnp.float32
    ) - jnp.dot(second.T, imag_w * first, precision=highest, preferred_element_type=jnp.float32)
    resid_real = resid_real.astype(jnp.bfloat16)
    resid_imag = resid_imag.astype(jnp.bfloat16)
    upper = jnp.concatenate([resid_real, -resid_imag], axis=1)
    lower = jnp.concatenate([resid_imag, resid_real], axis=1)
    return jnp.concatenate([upper, lower], axis=0)


def mix_kernel(depth, big_ref, recv_ref, out_ref, wide_ref, acc_ref):
    wide_ref[...] = recv_ref[...].astype(jnp.float32)
    big = big_ref[...]
    rows = big.shape[0]
    for r in range(depth):
        rhs = wide_ref[pl.ds(r, rows, stride=depth), :].astype(jnp.bfloat16)
        acc_ref[pl.ds(r, rows, stride=depth), :] = jnp.dot(
            big, rhs, preferred_element_type=jnp.float32
        )
    out_ref[...] = acc_ref[...].astype(out_ref.dtype)


def mix(big, recv, depth):
    total, lanes = recv.shape
    return pl.pallas_call(
        functools.partial(mix_kernel, depth),
        out_shape=jax.ShapeDtypeStruct((total, lanes), jnp.bfloat16),
        scratch_shapes=[
            pltpu.VMEM((total, lanes), jnp.float32),
            pltpu.VMEM((total, lanes), jnp.float32),
        ],
        cost_estimate=pl.CostEstimate(
            flops=2 * big.shape[0] * big.shape[1] * depth * lanes,
            bytes_accessed=4 * total * lanes,
            transcendentals=0,
        ),
    )(big, recv)


def source_kernel(owned, depth, meta_ref, recv_ref, noise_ref, lo_ref, hi_ref):
    pieces, _, lanes = recv_ref.shape
    half = depth // 2
    slab = meta_ref[0]
    row = lax.broadcasted_iota(jnp.int32, (depth, lanes), 0)
    lane = lax.broadcasted_iota(jnp.int32, (depth, lanes), 1)
    base = (slab * depth + row) * (pieces * lanes) + lane
    for b in range(owned):
        spot_at = meta_ref[2 + b]
        for part in range(2):
            start = (b * 2 + part) * depth
            for ct in range(pieces):
                cols = slice(ct * lanes, (ct + 1) * lanes)
                tile = recv_ref[ct, start : start + depth, :].astype(jnp.float32)
                value = noise_ref[:, cols] * tile
                if part == 0:
                    hit = base + ct * lanes == spot_at
                    value = value + jnp.where(hit, point_size, 0.0)
                lo_ref[b, part, :, cols] = value[:half]
                hi_ref[b, part, :, cols] = value[half:]


def sweep_kernel(depth, meta_ref, lo_ref, hi_ref, below_ref, above_ref, wave_ref, wbelow_ref,
                 wabove_ref, out_ref, are_ref, aim_ref, bre_ref, bim_ref, sre_ref, sim_ref, w_ref,
                 sr_ref, si_ref):
    half = depth // 2
    rows, cells = sre_ref.shape
    width = LANES
    chunks = cells // width
    slab = meta_ref[0]
    nslab = meta_ref[1]
    w_ref[0:HALO] = wbelow_ref[...]
    w_ref[HALO : HALO + depth] = wave_ref[...]
    w_ref[HALO + depth :] = wabove_ref[...]
    for part, dst in ((0, sre_ref), (1, sim_ref)):
        dst[0:HALO] = below_ref[0, part]
        dst[HALO : HALO + half] = lo_ref[0, part]
        dst[HALO + half : HALO + depth] = hi_ref[0, part]
        dst[HALO + depth :] = above_ref[0, part]
    zeros = jnp.zeros((rows, PAD), jnp.float32)
    for ref in (are_ref, aim_ref, bre_ref, bim_ref):
        ref[:, 0:PAD] = zeros
        ref[:, PAD + cells :] = zeros
    row = lax.broadcasted_iota(jnp.int32, (rows, width), 0)
    inside = jnp.logical_and(
        jnp.logical_or(row >= HALO, slab > 0),
        jnp.logical_or(row < HALO + depth, slab < nslab - 1),
    )

    def first(j, carry):
        c0 = pl.multiple_of(j * width, width)
        cols = pl.ds(c0, width)
        wave = w_ref[:, cols]
        diag_real = 6.0 - wave
        denom = diag_real * diag_real + damping * wave * (damping * wave)
        sr = jnp.where(inside, relaxation * diag_real / denom, 0.0)
        si = jnp.where(inside, relaxation * damping * wave / denom, 0.0)
        sr_ref[:, cols] = sr
        si_ref[:, cols] = si
        src_re = sre_ref[:, cols]
        src_im = sim_ref[:, cols]
        out = pl.ds(PAD + c0, width)
        are_ref[:, out] = sr * src_re - si * src_im
        aim_ref[:, out] = sr * src_im + si * src_re
        return carry

    lax.fori_loop(0, chunks, first, 0)

    keep = 1.0 - relaxation
    lane = lax.broadcasted_iota(jnp.int32, (rows, width), 1)
    col = jnp.bitwise_and(lane, GY - 1)
    has_ym = col != 0
    has_yp = col != GY - 1

    def sweep(src_pair, dst_pair, last):
        def chunk(j, carry):
            c0 = pl.multiple_of(j * width, width)
            cols = pl.ds(c0, width)

            def total(ref, src):
                ext = ref[:, pl.ds(c0, width + 2 * PAD)]
                rot = pltpu.roll(ext, GY, 1)
                mid = ext[:, PAD : PAD + width]
                xm = rot[:, PAD : PAD + width]
                xp = rot[:, 2 * PAD : 2 * PAD + width]
                ym = jnp.where(has_ym, pltpu.roll(mid, 1, 1), 0.0)
                yp = jnp.where(has_yp, pltpu.roll(mid, width - 1, 1), 0.0)
                dn = pltpu.roll(mid, 1, 0)
                up = pltpu.roll(mid, rows - 1, 0)
                return mid, src + (xm + xp + ym + yp + dn + up)

            re, t_re = total(src_pair[0], sre_ref[:, cols])
            im, t_im = total(src_pair[1], sim_ref[:, cols])
            s_r = sr_ref[:, cols]
            s_i = si_ref[:, cols]
            new_re = keep * re + (s_r * t_re - s_i * t_im)
            new_im = keep * im + (s_r * t_im + s_i * t_re)
            if last:
                out_ref[0, 0, :, cols] = new_re[HALO : HALO + depth]
                out_ref[1, 0, :, cols] = new_im[HALO : HALO + depth]
            else:
                dst_pair[0][:, pl.ds(PAD + c0, width)] = new_re
                dst_pair[1][:, pl.ds(PAD + c0, width)] = new_im
            return carry

        lax.fori_loop(0, chunks, chunk, 0)

    pairs = ((are_ref, aim_ref), (bre_ref, bim_ref))
    for k in range(SWEEPS - 1):
        sweep(pairs[k % 2], pairs[(k + 1) % 2], k == SWEEPS - 2)


def sweeps(meta, lo, hi, below, above, wave, wbelow, wabove):
    owned, _, half, cells = lo.shape
    depth = 2 * half
    rows = depth + 2 * HALO
    piece = pl.BlockSpec((1, 2, half, cells), lambda b, *_: (b, 0, 0, 0))
    halo = pl.BlockSpec((1, 2, HALO, cells), lambda b, *_: (b, 0, 0, 0))
    whole = lambda shape: pl.BlockSpec(shape, lambda b, *_: (0,) * len(shape))
    grid_spec = pltpu.PrefetchScalarGridSpec(
        num_scalar_prefetch=1,
        grid=(owned,),
        in_specs=[piece, piece, halo, halo, whole((depth, cells)), whole((HALO, cells)),
                  whole((HALO, cells))],
        out_specs=pl.BlockSpec((2, 1, depth, cells), lambda b, *_: (0, b, 0, 0)),
        scratch_shapes=[pltpu.VMEM((rows, cells + 2 * PAD), jnp.float32) for _ in range(4)]
        + [pltpu.VMEM((rows, cells), jnp.float32) for _ in range(5)],
    )
    return pl.pallas_call(
        functools.partial(sweep_kernel, depth),
        out_shape=jax.ShapeDtypeStruct((2, owned, depth, cells), jnp.float32),
        grid_spec=grid_spec,
        cost_estimate=pl.CostEstimate(
            flops=owned * SWEEPS * 60 * rows * cells,
            bytes_accessed=owned * 4 * cells * (6 * depth),
            transcendentals=0,
        ),
    )(meta, lo, hi, below, above, wave, wbelow, wabove)


def local(green_fields, pair_list, pair_values, noise_map, wave_square, station_cell):
    parts, owned, depth, cells = green_fields.shape
    nsta = lax.axis_size("sta")
    nslab = lax.axis_size("slab")
    count = owned * nsta
    lanes = cells // nsta
    slab = lax.axis_index("slab")
    up_pairs = [(i, i + 1) for i in range(nslab - 1)]
    down_pairs = [(i + 1, i) for i in range(nslab - 1)]
    half = depth // 2

    send = green_fields.reshape(parts, owned, depth, nsta, lanes)
    send = send.transpose(3, 0, 1, 2, 4).reshape(nsta, parts * owned * depth, lanes)
    recv = lax.all_to_all(send, "sta", 0, 0, tiled=True)

    big = build_resid(pair_list, pair_values, count)
    big = big.reshape(2, count, 2, nsta, owned).transpose(1, 0, 3, 2, 4)
    big = big.reshape(2 * count, 2 * count)
    big, wave_hi, wave_lo = lax.optimization_barrier(
        (big, wave_square[depth - HALO :], wave_square[:HALO])
    )
    wbelow = lax.ppermute(wave_hi, "slab", up_pairs)
    wabove = lax.ppermute(wave_lo, "slab", down_pairs)
    big, wbelow, wabove = lax.optimization_barrier((big, wbelow, wabove))
    mixed = mix(big, recv.reshape(nsta * parts * owned * depth, lanes), depth)
    back = lax.all_to_all(mixed.reshape(nsta, owned * parts * depth, lanes), "sta", 0, 0,
                          tiled=True)

    meta = jnp.concatenate(
        [jnp.stack([slab, jnp.int32(nslab)]).astype(jnp.int32), station_cell.astype(jnp.int32)]
    )
    lo, hi = pl.pallas_call(
        functools.partial(source_kernel, owned, depth),
        out_shape=[jax.ShapeDtypeStruct((owned, 2, half, cells), jnp.float32)] * 2,
        in_specs=[
            pl.BlockSpec(memory_space=pltpu.SMEM),
            pl.BlockSpec(memory_space=pltpu.VMEM),
            pl.BlockSpec(memory_space=pltpu.VMEM),
        ],
    )(meta, back, noise_map)
    below = lax.ppermute(hi, "slab", up_pairs)
    above = lax.ppermute(lo, "slab", down_pairs)
    return sweeps(meta, lo, hi, below, above, wave_square, wbelow, wabove)


def solution(mesh):
    placed = (P(None, "sta", "slab", None), P(), P(), P("slab", None), P("slab", None), P("sta"))
    return jax.shard_map(
        local, mesh=mesh, in_specs=placed, out_specs=P(None, "sta", "slab", None), check_vma=False
    )
```

```python
import functools

import jax
import jax.numpy as jnp
from jax import lax
from jax.experimental import pallas as pl
from jax.experimental.pallas import tpu as pltpu
from jax.sharding import PartitionSpec as P

GY = 64
SWEEPS = 6
HALO = 8

damping = 0.3
relaxation = 0.8
point_size = 2.0


def build_resid(pair_list, pair_values, count):
    labels = jnp.arange(count, dtype=jnp.int32)
    first = (pair_list[:, 0:1] == labels[None, :]).astype(jnp.float32)
    second = (pair_list[:, 1:2] == labels[None, :]).astype(jnp.float32)
    real_w = pair_values[0][:, None]
    imag_w = pair_values[1][:, None]
    highest = lax.Precision.HIGHEST
    resid_real = jnp.dot(
        first.T, real_w * second, precision=highest, preferred_element_type=jnp.float32
    ) + jnp.dot(second.T, real_w * first, precision=highest, preferred_element_type=jnp.float32)
    resid_imag = jnp.dot(
        first.T, imag_w * second, precision=highest, preferred_element_type=jnp.float32
    ) - jnp.dot(second.T, imag_w * first, precision=highest, preferred_element_type=jnp.float32)
    resid_real = resid_real.astype(jnp.bfloat16)
    resid_imag = resid_imag.astype(jnp.bfloat16)
    upper = jnp.concatenate([resid_real, -resid_imag], axis=1)
    lower = jnp.concatenate([resid_imag, resid_real], axis=1)
    return jnp.concatenate([upper, lower], axis=0)


def mix_kernel(depth, big_ref, recv_ref, out_ref, wide_ref, acc_ref):
    wide_ref[...] = recv_ref[...].astype(jnp.float32)
    big = big_ref[...]
    rows = big.shape[0]
    for r in range(depth):
        rhs = wide_ref[pl.ds(r, rows, stride=depth), :].astype(jnp.bfloat16)
        acc_ref[pl.ds(r, rows, stride=depth), :] = jnp.dot(
            big, rhs, preferred_element_type=jnp.float32
        )
    out_ref[...] = acc_ref[...].astype(out_ref.dtype)


def mix(big, recv, depth):
    total, lanes = recv.shape
    return pl.pallas_call(
        functools.partial(mix_kernel, depth),
        out_shape=jax.ShapeDtypeStruct((total, lanes), jnp.bfloat16),
        scratch_shapes=[
            pltpu.VMEM((total, lanes), jnp.float32),
            pltpu.VMEM((total, lanes), jnp.float32),
        ],
        cost_estimate=pl.CostEstimate(
            flops=2 * big.shape[0] * big.shape[1] * depth * lanes,
            bytes_accessed=4 * total * lanes,
            transcendentals=0,
        ),
    )(big, recv)


def source_kernel(owned, depth, meta_ref, recv_ref, noise_ref, lo_ref, hi_ref):
    pieces, _, lanes = recv_ref.shape
    half = depth // 2
    slab = meta_ref[0]
    row = lax.broadcasted_iota(jnp.int32, (depth, lanes), 0)
    lane = lax.broadcasted_iota(jnp.int32, (depth, lanes), 1)
    base = (slab * depth + row) * (pieces * lanes) + lane
    for b in range(owned):
        spot_at = meta_ref[2 + b]
        for part in range(2):
            start = (b * 2 + part) * depth
            for ct in range(pieces):
                cols = slice(ct * lanes, (ct + 1) * lanes)
                tile = recv_ref[ct, start : start + depth, :].astype(jnp.float32)
                value = noise_ref[:, cols] * tile
                if part == 0:
                    hit = base + ct * lanes == spot_at
                    value = value + jnp.where(hit, point_size, 0.0)
                lo_ref[b, part, :, cols] = value[:half]
                hi_ref[b, part, :, cols] = value[half:]


def sweep_kernel(depth, meta_ref, lo_ref, hi_ref, below_ref, above_ref, wave_ref, wbelow_ref,
                 wabove_ref, out_ref, re_ref, im_ref, sre_ref, sim_ref, w_ref, sr_ref, si_ref):
    half = depth // 2
    rows, cells = re_ref.shape
    slab = meta_ref[0]
    nslab = meta_ref[1]
    w_ref[0:HALO] = wbelow_ref[...]
    w_ref[HALO : HALO + depth] = wave_ref[...]
    w_ref[HALO + depth :] = wabove_ref[...]
    for part, dst in ((0, sre_ref), (1, sim_ref)):
        dst[0:HALO] = below_ref[0, part]
        dst[HALO : HALO + half] = lo_ref[0, part]
        dst[HALO + half : HALO + depth] = hi_ref[0, part]
        dst[HALO + depth :] = above_ref[0, part]
    wave = w_ref[...]
    row = lax.broadcasted_iota(jnp.int32, (rows, cells), 0)
    inside = jnp.logical_and(
        jnp.logical_or(row >= HALO, slab > 0),
        jnp.logical_or(row < HALO + depth, slab < nslab - 1),
    )
    diag_real = 6.0 - wave
    denom = diag_real * diag_real + damping * wave * (damping * wave)
    sr_ref[...] = jnp.where(inside, relaxation * diag_real / denom, 0.0)
    si_ref[...] = jnp.where(inside, relaxation * damping * wave / denom, 0.0)
    sr = sr_ref[...]
    si = si_ref[...]
    src_re = sre_ref[...]
    src_im = sim_ref[...]
    re_ref[...] = sr * src_re - si * src_im
    im_ref[...] = sr * src_im + si * src_re

    keep = 1.0 - relaxation

    def body(_, carry):
        lane = lax.broadcasted_iota(jnp.int32, (rows, cells), 1)
        col = jnp.bitwise_and(lane, GY - 1)
        has_xm = lane >= GY
        has_xp = lane < cells - GY
        has_ym = col != 0
        has_yp = col != GY - 1

        def total(f, src):
            shifted = pltpu.roll(f, GY, 1)
            xm = jnp.where(has_xm, shifted, 0.0)
            xp = jnp.where(has_xp, pltpu.roll(shifted, cells - 2 * GY, 1), 0.0)
            ym = jnp.where(has_ym, pltpu.roll(f, 1, 1), 0.0)
            yp = jnp.where(has_yp, pltpu.roll(f, cells - 1, 1), 0.0)
            dn = pltpu.roll(f, 1, 0)
            up = pltpu.roll(f, rows - 1, 0)
            return src + (xm + xp + ym + yp + dn + up)

        re = re_ref[...]
        im = im_ref[...]
        t_re = total(re, sre_ref[...])
        t_im = total(im, sim_ref[...])
        s_r = sr_ref[...]
        s_i = si_ref[...]
        re_ref[...] = keep * re + (s_r * t_re - s_i * t_im)
        im_ref[...] = keep * im + (s_r * t_im + s_i * t_re)
        return carry

    lax.fori_loop(0, SWEEPS - 1, body, 0)
    out_ref[0, 0] = re_ref[HALO : HALO + depth]
    out_ref[1, 0] = im_ref[HALO : HALO + depth]


def sweeps(meta, lo, hi, below, above, wave, wbelow, wabove):
    owned, _, half, cells = lo.shape
    depth = 2 * half
    rows = depth + 2 * HALO
    piece = pl.BlockSpec((1, 2, half, cells), lambda b, *_: (b, 0, 0, 0))
    halo = pl.BlockSpec((1, 2, HALO, cells), lambda b, *_: (b, 0, 0, 0))
    whole = lambda shape: pl.BlockSpec(shape, lambda b, *_: (0,) * len(shape))
    grid_spec = pltpu.PrefetchScalarGridSpec(
        num_scalar_prefetch=1,
        grid=(owned,),
        in_specs=[piece, piece, halo, halo, whole((depth, cells)), whole((HALO, cells)),
                  whole((HALO, cells))],
        out_specs=pl.BlockSpec((2, 1, depth, cells), lambda b, *_: (0, b, 0, 0)),
        scratch_shapes=[pltpu.VMEM((rows, cells), jnp.float32) for _ in range(7)],
    )
    return pl.pallas_call(
        functools.partial(sweep_kernel, depth),
        out_shape=jax.ShapeDtypeStruct((2, owned, depth, cells), jnp.float32),
        grid_spec=grid_spec,
        cost_estimate=pl.CostEstimate(
            flops=owned * SWEEPS * 90 * rows * cells,
            bytes_accessed=owned * 4 * cells * (6 * depth),
            transcendentals=0,
        ),
    )(meta, lo, hi, below, above, wave, wbelow, wabove)


def local(green_fields, pair_list, pair_values, noise_map, wave_square, station_cell):
    parts, owned, depth, cells = green_fields.shape
    nsta = lax.axis_size("sta")
    nslab = lax.axis_size("slab")
    count = owned * nsta
    lanes = cells // nsta
    slab = lax.axis_index("slab")
    up_pairs = [(i, i + 1) for i in range(nslab - 1)]
    down_pairs = [(i + 1, i) for i in range(nslab - 1)]
    half = depth // 2

    send = green_fields.reshape(parts, owned, depth, nsta, lanes)
    send = send.transpose(3, 0, 1, 2, 4).reshape(nsta, parts * owned * depth, lanes)
    recv = lax.all_to_all(send, "sta", 0, 0, tiled=True)

    big = build_resid(pair_list, pair_values, count)
    big = big.reshape(2, count, 2, nsta, owned).transpose(1, 0, 3, 2, 4)
    big = big.reshape(2 * count, 2 * count)
    big, wave_hi, wave_lo = lax.optimization_barrier(
        (big, wave_square[depth - HALO :], wave_square[:HALO])
    )
    wbelow = lax.ppermute(wave_hi, "slab", up_pairs)
    wabove = lax.ppermute(wave_lo, "slab", down_pairs)
    big, wbelow, wabove = lax.optimization_barrier((big, wbelow, wabove))
    mixed = mix(big, recv.reshape(nsta * parts * owned * depth, lanes), depth)
    back = lax.all_to_all(mixed.reshape(nsta, owned * parts * depth, lanes), "sta", 0, 0,
                          tiled=True)

    meta = jnp.concatenate(
        [jnp.stack([slab, jnp.int32(nslab)]).astype(jnp.int32), station_cell.astype(jnp.int32)]
    )
    lo, hi = pl.pallas_call(
        functools.partial(source_kernel, owned, depth),
        out_shape=[jax.ShapeDtypeStruct((owned, 2, half, cells), jnp.float32)] * 2,
        in_specs=[
            pl.BlockSpec(memory_space=pltpu.SMEM),
            pl.BlockSpec(memory_space=pltpu.VMEM),
            pl.BlockSpec(memory_space=pltpu.VMEM),
        ],
    )(meta, back, noise_map)
    below = lax.ppermute(hi, "slab", up_pairs)
    above = lax.ppermute(lo, "slab", down_pairs)
    return sweeps(meta, lo, hi, below, above, wave_square, wbelow, wabove)


def solution(mesh):
    placed = (P(None, "sta", "slab", None), P(), P(), P("slab", None), P("slab", None), P("sta"))
    return jax.shard_map(
        local, mesh=mesh, in_specs=placed, out_specs=P(None, "sta", "slab", None), check_vma=False
    )
```

```python
import functools

import jax
import jax.numpy as jnp
from jax import lax
from jax.experimental import pallas as pl
from jax.experimental.pallas import tpu as pltpu
from jax.sharding import PartitionSpec as P

GY = 64
SWEEPS = 6
HALO = 8
LANES = 512
PAD = 128

damping = 0.3
relaxation = 0.8
point_size = 2.0


def build_resid(pair_list, pair_values, count):
    labels = jnp.arange(count, dtype=jnp.int32)
    first = (pair_list[:, 0:1] == labels[None, :]).astype(jnp.float32)
    second = (pair_list[:, 1:2] == labels[None, :]).astype(jnp.float32)
    real_w = pair_values[0][:, None]
    imag_w = pair_values[1][:, None]
    highest = lax.Precision.HIGHEST
    resid_real = jnp.dot(
        first.T, real_w * second, precision=highest, preferred_element_type=jnp.float32
    ) + jnp.dot(second.T, real_w * first, precision=highest, preferred_element_type=jnp.float32)
    resid_imag = jnp.dot(
        first.T, imag_w * second, precision=highest, preferred_element_type=jnp.float32
    ) - jnp.dot(second.T, imag_w * first, precision=highest, preferred_element_type=jnp.float32)
    resid_real = resid_real.astype(jnp.bfloat16)
    resid_imag = resid_imag.astype(jnp.bfloat16)
    upper = jnp.concatenate([resid_real, -resid_imag], axis=1)
    lower = jnp.concatenate([resid_imag, resid_real], axis=1)
    return jnp.concatenate([upper, lower], axis=0)


def mix_kernel(depth, big_ref, recv_ref, out_ref, wide_ref, acc_ref):
    wide_ref[...] = recv_ref[...].astype(jnp.float32)
    big = big_ref[...]
    rows = big.shape[0]
    for r in range(depth):
        rhs = wide_ref[pl.ds(r, rows, stride=depth), :].astype(jnp.bfloat16)
        acc_ref[pl.ds(r, rows, stride=depth), :] = jnp.dot(
            big, rhs, preferred_element_type=jnp.float32
        )
    out_ref[...] = acc_ref[...].astype(out_ref.dtype)


def mix(big, recv, depth):
    total, lanes = recv.shape
    return pl.pallas_call(
        functools.partial(mix_kernel, depth),
        out_shape=jax.ShapeDtypeStruct((total, lanes), jnp.bfloat16),
        scratch_shapes=[
            pltpu.VMEM((total, lanes), jnp.float32),
            pltpu.VMEM((total, lanes), jnp.float32),
        ],
        cost_estimate=pl.CostEstimate(
            flops=2 * big.shape[0] * big.shape[1] * depth * lanes,
            bytes_accessed=4 * total * lanes,
            transcendentals=0,
        ),
    )(big, recv)


def source_kernel(owned, depth, meta_ref, recv_ref, noise_ref, lo_ref, hi_ref):
    pieces, _, lanes = recv_ref.shape
    half = depth // 2
    slab = meta_ref[0]
    row = lax.broadcasted_iota(jnp.int32, (depth, lanes), 0)
    lane = lax.broadcasted_iota(jnp.int32, (depth, lanes), 1)
    base = (slab * depth + row) * (pieces * lanes) + lane
    for b in range(owned):
        spot_at = meta_ref[2 + b]
        for part in range(2):
            start = (b * 2 + part) * depth
            for ct in range(pieces):
                cols = slice(ct * lanes, (ct + 1) * lanes)
                tile = recv_ref[ct, start : start + depth, :].astype(jnp.float32)
                value = noise_ref[:, cols] * tile
                if part == 0:
                    hit = base + ct * lanes == spot_at
                    value = value + jnp.where(hit, point_size, 0.0)
                lo_ref[b, part, :, cols] = value[:half]
                hi_ref[b, part, :, cols] = value[half:]


def sweep_kernel(depth, meta_ref, lo_ref, hi_ref, below_ref, above_ref, wave_ref, wbelow_ref,
                 wabove_ref, out_ref, are_ref, aim_ref, bre_ref, bim_ref, sre_ref, sim_ref, w_ref,
                 sr_ref, si_ref):
    half = depth // 2
    rows, cells = sre_ref.shape
    width = LANES
    chunks = cells // width
    slab = meta_ref[0]
    nslab = meta_ref[1]
    w_ref[0:HALO] = wbelow_ref[...]
    w_ref[HALO : HALO + depth] = wave_ref[...]
    w_ref[HALO + depth :] = wabove_ref[...]
    for part, dst in ((0, sre_ref), (1, sim_ref)):
        dst[0:HALO] = below_ref[0, part]
        dst[HALO : HALO + half] = lo_ref[0, part]
        dst[HALO + half : HALO + depth] = hi_ref[0, part]
        dst[HALO + depth :] = above_ref[0, part]
    zeros = jnp.zeros((rows, PAD), jnp.float32)
    for ref in (are_ref, aim_ref, bre_ref, bim_ref):
        ref[:, 0:PAD] = zeros
        ref[:, PAD + cells :] = zeros
    row = lax.broadcasted_iota(jnp.int32, (rows, width), 0)
    inside = jnp.logical_and(
        jnp.logical_or(row >= HALO, slab > 0),
        jnp.logical_or(row < HALO + depth, slab < nslab - 1),
    )

    def first(j, carry):
        c0 = pl.multiple_of(j * width, width)
        cols = pl.ds(c0, width)
        wave = w_ref[:, cols]
        diag_real = 6.0 - wave
        denom = diag_real * diag_real + damping * wave * (damping * wave)
        sr = jnp.where(inside, relaxation * diag_real / denom, 0.0)
        si = jnp.where(inside, relaxation * damping * wave / denom, 0.0)
        sr_ref[:, cols] = sr
        si_ref[:, cols] = si
        src_re = sre_ref[:, cols]
        src_im = sim_ref[:, cols]
        out = pl.ds(PAD + c0, width)
        are_ref[:, out] = sr * src_re - si * src_im
        aim_ref[:, out] = sr * src_im + si * src_re
        return carry

    lax.fori_loop(0, chunks, first, 0)

    keep = 1.0 - relaxation
    lane = lax.broadcasted_iota(jnp.int32, (rows, width), 1)
    col = jnp.bitwise_and(lane, GY - 1)
    has_ym = col != 0
    has_yp = col != GY - 1

    def sweep(src_pair, dst_pair, last):
        def chunk(j, carry):
            c0 = pl.multiple_of(j * width, width)
            cols = pl.ds(c0, width)

            def total(ref, src):
                ext = ref[:, pl.ds(c0, width + 2 * PAD)]
                rot = pltpu.roll(ext, GY, 1)
                mid = ext[:, PAD : PAD + width]
                xm = rot[:, PAD : PAD + width]
                xp = rot[:, 2 * PAD : 2 * PAD + width]
                ym = jnp.where(has_ym, pltpu.roll(mid, 1, 1), 0.0)
                yp = jnp.where(has_yp, pltpu.roll(mid, width - 1, 1), 0.0)
                dn = pltpu.roll(mid, 1, 0)
                up = pltpu.roll(mid, rows - 1, 0)
                return mid, src + (xm + xp + ym + yp + dn + up)

            re, t_re = total(src_pair[0], sre_ref[:, cols])
            im, t_im = total(src_pair[1], sim_ref[:, cols])
            s_r = sr_ref[:, cols]
            s_i = si_ref[:, cols]
            new_re = keep * re + (s_r * t_re - s_i * t_im)
            new_im = keep * im + (s_r * t_im + s_i * t_re)
            if last:
                out_ref[0, 0, :, cols] = new_re[HALO : HALO + depth]
                out_ref[1, 0, :, cols] = new_im[HALO : HALO + depth]
            else:
                dst_pair[0][:, pl.ds(PAD + c0, width)] = new_re
                dst_pair[1][:, pl.ds(PAD + c0, width)] = new_im
            return carry

        lax.fori_loop(0, chunks, chunk, 0, unroll=True)

    pairs = ((are_ref, aim_ref), (bre_ref, bim_ref))
    for k in range(SWEEPS - 1):
        sweep(pairs[k % 2], pairs[(k + 1) % 2], k == SWEEPS - 2)


def sweeps(meta, lo, hi, below, above, wave, wbelow, wabove):
    owned, _, half, cells = lo.shape
    depth = 2 * half
    rows = depth + 2 * HALO
    piece = pl.BlockSpec((1, 2, half, cells), lambda b, *_: (b, 0, 0, 0))
    halo = pl.BlockSpec((1, 2, HALO, cells), lambda b, *_: (b, 0, 0, 0))
    whole = lambda shape: pl.BlockSpec(shape, lambda b, *_: (0,) * len(shape))
    grid_spec = pltpu.PrefetchScalarGridSpec(
        num_scalar_prefetch=1,
        grid=(owned,),
        in_specs=[piece, piece, halo, halo, whole((depth, cells)), whole((HALO, cells)),
                  whole((HALO, cells))],
        out_specs=pl.BlockSpec((2, 1, depth, cells), lambda b, *_: (0, b, 0, 0)),
        scratch_shapes=[pltpu.VMEM((rows, cells + 2 * PAD), jnp.float32) for _ in range(4)]
        + [pltpu.VMEM((rows, cells), jnp.float32) for _ in range(5)],
    )
    return pl.pallas_call(
        functools.partial(sweep_kernel, depth),
        out_shape=jax.ShapeDtypeStruct((2, owned, depth, cells), jnp.float32),
        grid_spec=grid_spec,
        cost_estimate=pl.CostEstimate(
            flops=owned * SWEEPS * 60 * rows * cells,
            bytes_accessed=owned * 4 * cells * (6 * depth),
            transcendentals=0,
        ),
    )(meta, lo, hi, below, above, wave, wbelow, wabove)


def local(green_fields, pair_list, pair_values, noise_map, wave_square, station_cell):
    parts, owned, depth, cells = green_fields.shape
    nsta = lax.axis_size("sta")
    nslab = lax.axis_size("slab")
    count = owned * nsta
    lanes = cells // nsta
    slab = lax.axis_index("slab")
    up_pairs = [(i, i + 1) for i in range(nslab - 1)]
    down_pairs = [(i + 1, i) for i in range(nslab - 1)]
    half = depth // 2

    send = green_fields.reshape(parts, owned, depth, nsta, lanes)
    send = send.transpose(3, 0, 1, 2, 4).reshape(nsta, parts * owned * depth, lanes)
    recv = lax.all_to_all(send, "sta", 0, 0, tiled=True)

    big = build_resid(pair_list, pair_values, count)
    big = big.reshape(2, count, 2, nsta, owned).transpose(1, 0, 3, 2, 4)
    big = big.reshape(2 * count, 2 * count)
    big, wave_hi, wave_lo = lax.optimization_barrier(
        (big, wave_square[depth - HALO :], wave_square[:HALO])
    )
    wbelow = lax.ppermute(wave_hi, "slab", up_pairs)
    wabove = lax.ppermute(wave_lo, "slab", down_pairs)
    big, wbelow, wabove = lax.optimization_barrier((big, wbelow, wabove))
    mixed = mix(big, recv.reshape(nsta * parts * owned * depth, lanes), depth)
    back = lax.all_to_all(mixed.reshape(nsta, owned * parts * depth, lanes), "sta", 0, 0,
                          tiled=True)

    meta = jnp.concatenate(
        [jnp.stack([slab, jnp.int32(nslab)]).astype(jnp.int32), station_cell.astype(jnp.int32)]
    )
    lo, hi = pl.pallas_call(
        functools.partial(source_kernel, owned, depth),
        out_shape=[jax.ShapeDtypeStruct((owned, 2, half, cells), jnp.float32)] * 2,
        in_specs=[
            pl.BlockSpec(memory_space=pltpu.SMEM),
            pl.BlockSpec(memory_space=pltpu.VMEM),
            pl.BlockSpec(memory_space=pltpu.VMEM),
        ],
    )(meta, back, noise_map)
    below = lax.ppermute(hi, "slab", up_pairs)
    above = lax.ppermute(lo, "slab", down_pairs)
    return sweeps(meta, lo, hi, below, above, wave_square, wbelow, wabove)


def solution(mesh):
    placed = (P(None, "sta", "slab", None), P(), P(), P("slab", None), P("slab", None), P("sta"))
    return jax.shard_map(
        local, mesh=mesh, in_specs=placed, out_specs=P(None, "sta", "slab", None), check_vma=False
    )
```

```python
import functools

import jax
import jax.numpy as jnp
from jax import lax
from jax.experimental import pallas as pl
from jax.experimental.pallas import tpu as pltpu
from jax.sharding import PartitionSpec as P

GY = 64
SWEEPS = 6
HALO = 8
LANES = 512
PAD = 128

damping = 0.3
relaxation = 0.8
point_size = 2.0


def build_resid(pair_list, pair_values, count):
    labels = jnp.arange(count, dtype=jnp.int32)
    first = (pair_list[:, 0:1] == labels[None, :]).astype(jnp.float32)
    second = (pair_list[:, 1:2] == labels[None, :]).astype(jnp.float32)
    real_w = pair_values[0][:, None]
    imag_w = pair_values[1][:, None]
    highest = lax.Precision.HIGHEST
    resid_real = jnp.dot(
        first.T, real_w * second, precision=highest, preferred_element_type=jnp.float32
    ) + jnp.dot(second.T, real_w * first, precision=highest, preferred_element_type=jnp.float32)
    resid_imag = jnp.dot(
        first.T, imag_w * second, precision=highest, preferred_element_type=jnp.float32
    ) - jnp.dot(second.T, imag_w * first, precision=highest, preferred_element_type=jnp.float32)
    resid_real = resid_real.astype(jnp.bfloat16)
    resid_imag = resid_imag.astype(jnp.bfloat16)
    upper = jnp.concatenate([resid_real, -resid_imag], axis=1)
    lower = jnp.concatenate([resid_imag, resid_real], axis=1)
    return jnp.concatenate([upper, lower], axis=0)


def mix_kernel(depth, big_ref, recv_ref, out_ref, wide_ref, acc_ref):
    wide_ref[...] = recv_ref[...].astype(jnp.float32)
    big = big_ref[...]
    rows = big.shape[0]
    for r in range(depth):
        rhs = wide_ref[pl.ds(r, rows, stride=depth), :].astype(jnp.bfloat16)
        acc_ref[pl.ds(r, rows, stride=depth), :] = jnp.dot(
            big, rhs, preferred_element_type=jnp.float32
        )
    out_ref[...] = acc_ref[...].astype(out_ref.dtype)


def mix(big, recv, depth):
    total, lanes = recv.shape
    return pl.pallas_call(
        functools.partial(mix_kernel, depth),
        out_shape=jax.ShapeDtypeStruct((total, lanes), jnp.bfloat16),
        scratch_shapes=[
            pltpu.VMEM((total, lanes), jnp.float32),
            pltpu.VMEM((total, lanes), jnp.float32),
        ],
        cost_estimate=pl.CostEstimate(
            flops=2 * big.shape[0] * big.shape[1] * depth * lanes,
            bytes_accessed=4 * total * lanes,
            transcendentals=0,
        ),
    )(big, recv)


def source_kernel(depth, b, meta_ref, recv_ref, noise_ref, lo_ref, hi_ref):
    pieces, _, lanes = recv_ref.shape
    half = depth // 2
    slab = meta_ref[0]
    spot_at = meta_ref[2 + b]
    row = lax.broadcasted_iota(jnp.int32, (depth, lanes), 0)
    lane = lax.broadcasted_iota(jnp.int32, (depth, lanes), 1)
    base = (slab * depth + row) * (pieces * lanes) + lane
    for part in range(2):
        for ct in range(pieces):
            cols = slice(ct * lanes, (ct + 1) * lanes)
            tile = recv_ref[ct, part * depth : (part + 1) * depth, :].astype(jnp.float32)
            value = noise_ref[:, cols] * tile
            if part == 0:
                hit = base + ct * lanes == spot_at
                value = value + jnp.where(hit, point_size, 0.0)
            lo_ref[0, part, :, cols] = value[:half]
            hi_ref[0, part, :, cols] = value[half:]


def sweep_kernel(depth, aliased, meta_ref, lo_ref, hi_ref, below_ref, above_ref, wave_ref,
                 wbelow_ref, wabove_ref, *refs):
    if aliased:
        refs = refs[1:]
    out_ref, are_ref, aim_ref, bre_ref, bim_ref, sre_ref, sim_ref, w_ref, sr_ref, si_ref = refs
    half = depth // 2
    rows, cells = sre_ref.shape
    width = LANES
    chunks = cells // width
    slab = meta_ref[0]
    nslab = meta_ref[1]
    w_ref[0:HALO] = wbelow_ref[...]
    w_ref[HALO : HALO + depth] = wave_ref[...]
    w_ref[HALO + depth :] = wabove_ref[...]
    for part, dst in ((0, sre_ref), (1, sim_ref)):
        dst[0:HALO] = below_ref[0, part]
        dst[HALO : HALO + half] = lo_ref[0, part]
        dst[HALO + half : HALO + depth] = hi_ref[0, part]
        dst[HALO + depth :] = above_ref[0, part]
    zeros = jnp.zeros((rows, PAD), jnp.float32)
    for ref in (are_ref, aim_ref, bre_ref, bim_ref):
        ref[:, 0:PAD] = zeros
        ref[:, PAD + cells :] = zeros
    row = lax.broadcasted_iota(jnp.int32, (rows, width), 0)
    inside = jnp.logical_and(
        jnp.logical_or(row >= HALO, slab > 0),
        jnp.logical_or(row < HALO + depth, slab < nslab - 1),
    )

    def first(j, carry):
        c0 = pl.multiple_of(j * width, width)
        cols = pl.ds(c0, width)
        wave = w_ref[:, cols]
        diag_real = 6.0 - wave
        denom = diag_real * diag_real + damping * wave * (damping * wave)
        sr = jnp.where(inside, relaxation * diag_real / denom, 0.0)
        si = jnp.where(inside, relaxation * damping * wave / denom, 0.0)
        sr_ref[:, cols] = sr
        si_ref[:, cols] = si
        src_re = sre_ref[:, cols]
        src_im = sim_ref[:, cols]
        out = pl.ds(PAD + c0, width)
        are_ref[:, out] = sr * src_re - si * src_im
        aim_ref[:, out] = sr * src_im + si * src_re
        return carry

    lax.fori_loop(0, chunks, first, 0)

    keep = 1.0 - relaxation
    lane = lax.broadcasted_iota(jnp.int32, (rows, width), 1)
    col = jnp.bitwise_and(lane, GY - 1)
    has_ym = col != 0
    has_yp = col != GY - 1

    def sweep(src_pair, dst_pair, last):
        def chunk(j, carry):
            c0 = pl.multiple_of(j * width, width)
            cols = pl.ds(c0, width)

            def total(ref, src):
                ext = ref[:, pl.ds(c0, width + 2 * PAD)]
                rot = pltpu.roll(ext, GY, 1)
                mid = ext[:, PAD : PAD + width]
                xm = rot[:, PAD : PAD + width]
                xp = rot[:, 2 * PAD : 2 * PAD + width]
                ym = jnp.where(has_ym, pltpu.roll(mid, 1, 1), 0.0)
                yp = jnp.where(has_yp, pltpu.roll(mid, width - 1, 1), 0.0)
                dn = pltpu.roll(mid, 1, 0)
                up = pltpu.roll(mid, rows - 1, 0)
                return mid, src + (xm + xp + ym + yp + dn + up)

            re, t_re = total(src_pair[0], sre_ref[:, cols])
            im, t_im = total(src_pair[1], sim_ref[:, cols])
            s_r = sr_ref[:, cols]
            s_i = si_ref[:, cols]
            new_re = keep * re + (s_r * t_re - s_i * t_im)
            new_im = keep * im + (s_r * t_im + s_i * t_re)
            if last:
                out_ref[0, 0, :, cols] = new_re[HALO : HALO + depth]
                out_ref[1, 0, :, cols] = new_im[HALO : HALO + depth]
            else:
                dst_pair[0][:, pl.ds(PAD + c0, width)] = new_re
                dst_pair[1][:, pl.ds(PAD + c0, width)] = new_im
            return carry

        lax.fori_loop(0, chunks, chunk, 0, unroll=True)

    pairs = ((are_ref, aim_ref), (bre_ref, bim_ref))
    for k in range(SWEEPS - 1):
        sweep(pairs[k % 2], pairs[(k + 1) % 2], k == SWEEPS - 2)


def sweeps(meta, lo, hi, below, above, wave, wbelow, wabove, b, owned, prev):
    _, _, half, cells = lo.shape
    depth = 2 * half
    rows = depth + 2 * HALO
    piece = pl.BlockSpec((1, 2, half, cells), lambda i, *_: (0, 0, 0, 0))
    halo = pl.BlockSpec((1, 2, HALO, cells), lambda i, *_: (0, 0, 0, 0))
    whole = lambda shape: pl.BlockSpec(shape, lambda i, *_: (0,) * len(shape))
    in_specs = [piece, piece, halo, halo, whole((depth, cells)), whole((HALO, cells)),
                whole((HALO, cells))]
    operands = [meta, lo, hi, below, above, wave, wbelow, wabove]
    aliases = {}
    if prev is not None:
        in_specs.append(pl.BlockSpec(memory_space=pl.ANY))
        aliases = {len(operands): 0}
        operands.append(prev)
    grid_spec = pltpu.PrefetchScalarGridSpec(
        num_scalar_prefetch=1,
        grid=(1,),
        in_specs=in_specs,
        out_specs=pl.BlockSpec((2, 1, depth, cells), lambda i, *_: (0, b, 0, 0)),
        scratch_shapes=[pltpu.VMEM((rows, cells + 2 * PAD), jnp.float32) for _ in range(4)]
        + [pltpu.VMEM((rows, cells), jnp.float32) for _ in range(5)],
    )
    return pl.pallas_call(
        functools.partial(sweep_kernel, depth, prev is not None),
        out_shape=jax.ShapeDtypeStruct((2, owned, depth, cells), jnp.float32),
        grid_spec=grid_spec,
        input_output_aliases=aliases,
        cost_estimate=pl.CostEstimate(
            flops=SWEEPS * 60 * rows * cells,
            bytes_accessed=4 * cells * (6 * depth),
            transcendentals=0,
        ),
    )(*operands)


def local(green_fields, pair_list, pair_values, noise_map, wave_square, station_cell):
    parts, owned, depth, cells = green_fields.shape
    nsta = lax.axis_size("sta")
    nslab = lax.axis_size("slab")
    count = owned * nsta
    lanes = cells // nsta
    slab = lax.axis_index("slab")
    up_pairs = [(i, i + 1) for i in range(nslab - 1)]
    down_pairs = [(i + 1, i) for i in range(nslab - 1)]
    half = depth // 2

    send = green_fields.reshape(parts, owned, depth, nsta, lanes)
    send = send.transpose(3, 0, 1, 2, 4).reshape(nsta, parts * owned * depth, lanes)
    recv = lax.all_to_all(send, "sta", 0, 0, tiled=True)

    big = build_resid(pair_list, pair_values, count)
    big = big.reshape(2, nsta, owned, 2, nsta, owned).transpose(2, 1, 0, 4, 3, 5)
    big = big.reshape(2 * count, 2 * count)
    big, wave_hi, wave_lo = lax.optimization_barrier(
        (big, wave_square[depth - HALO :], wave_square[:HALO])
    )
    wbelow = lax.ppermute(wave_hi, "slab", up_pairs)
    wabove = lax.ppermute(wave_lo, "slab", down_pairs)
    big, wbelow, wabove = lax.optimization_barrier((big, wbelow, wabove))
    mixed = mix(big, recv.reshape(nsta * parts * owned * depth, lanes), depth)
    mixed = mixed.reshape(owned, nsta, parts * depth, lanes)
    meta = jnp.concatenate(
        [jnp.stack([slab, jnp.int32(nslab)]).astype(jnp.int32), station_cell.astype(jnp.int32)]
    )
    out = None
    for b in range(owned):
        back = lax.all_to_all(mixed[b], "sta", 0, 0, tiled=True)
        lo, hi = pl.pallas_call(
            functools.partial(source_kernel, depth, b),
            out_shape=[jax.ShapeDtypeStruct((1, 2, half, cells), jnp.float32)] * 2,
            in_specs=[
                pl.BlockSpec(memory_space=pltpu.SMEM),
                pl.BlockSpec(memory_space=pltpu.VMEM),
                pl.BlockSpec(memory_space=pltpu.VMEM),
            ],
        )(meta, back, noise_map)
        below = lax.ppermute(hi, "slab", up_pairs)
        above = lax.ppermute(lo, "slab", down_pairs)
        out = sweeps(meta, lo, hi, below, above, wave_square, wbelow, wabove, b, owned, out)
    return out


def solution(mesh):
    placed = (P(None, "sta", "slab", None), P(), P(), P("slab", None), P("slab", None), P("sta"))
    return jax.shard_map(
        local, mesh=mesh, in_specs=placed, out_specs=P(None, "sta", "slab", None), check_vma=False
    )
```

```python
import functools

import jax
import jax.numpy as jnp
from jax import lax
from jax.experimental import pallas as pl
from jax.experimental.pallas import tpu as pltpu
from jax.sharding import PartitionSpec as P

GY = 64
SWEEPS = 6
HALO = 8
LANES = 512
PAD = 128

damping = 0.3
relaxation = 0.8
point_size = 2.0


def build_resid(pair_list, pair_values, count):
    labels = jnp.arange(count, dtype=jnp.int32)
    first = (pair_list[:, 0:1] == labels[None, :]).astype(jnp.float32)
    second = (pair_list[:, 1:2] == labels[None, :]).astype(jnp.float32)
    real_w = pair_values[0][:, None]
    imag_w = pair_values[1][:, None]
    highest = lax.Precision.HIGHEST
    resid_real = jnp.dot(
        first.T, real_w * second, precision=highest, preferred_element_type=jnp.float32
    ) + jnp.dot(second.T, real_w * first, precision=highest, preferred_element_type=jnp.float32)
    resid_imag = jnp.dot(
        first.T, imag_w * second, precision=highest, preferred_element_type=jnp.float32
    ) - jnp.dot(second.T, imag_w * first, precision=highest, preferred_element_type=jnp.float32)
    resid_real = resid_real.astype(jnp.bfloat16)
    resid_imag = resid_imag.astype(jnp.bfloat16)
    upper = jnp.concatenate([resid_real, -resid_imag], axis=1)
    lower = jnp.concatenate([resid_imag, resid_real], axis=1)
    return jnp.concatenate([upper, lower], axis=0)


def mix_kernel(depth, big_ref, recv_ref, out_ref, wide_ref, acc_ref):
    wide_ref[...] = recv_ref[...].astype(jnp.float32)
    big = big_ref[...]
    rows = big.shape[0]
    for r in range(depth):
        rhs = wide_ref[pl.ds(r, rows, stride=depth), :].astype(jnp.bfloat16)
        acc_ref[pl.ds(r, rows, stride=depth), :] = jnp.dot(
            big, rhs, preferred_element_type=jnp.float32
        )
    out_ref[...] = acc_ref[...].astype(out_ref.dtype)


def mix(big, recv, depth):
    total, lanes = recv.shape
    return pl.pallas_call(
        functools.partial(mix_kernel, depth),
        out_shape=jax.ShapeDtypeStruct((total, lanes), jnp.bfloat16),
        scratch_shapes=[
            pltpu.VMEM((total, lanes), jnp.float32),
            pltpu.VMEM((total, lanes), jnp.float32),
        ],
        cost_estimate=pl.CostEstimate(
            flops=2 * big.shape[0] * big.shape[1] * depth * lanes,
            bytes_accessed=4 * total * lanes,
            transcendentals=0,
        ),
    )(big, recv)


def source_kernel(owned, depth, meta_ref, recv_ref, noise_ref, lo_ref, hi_ref):
    pieces, _, lanes = recv_ref.shape
    half = depth // 2
    slab = meta_ref[0]
    row = lax.broadcasted_iota(jnp.int32, (depth, lanes), 0)
    lane = lax.broadcasted_iota(jnp.int32, (depth, lanes), 1)
    base = (slab * depth + row) * (pieces * lanes) + lane
    for b in range(owned):
        spot_at = meta_ref[2 + b]
        for part in range(2):
            start = (b * 2 + part) * depth
            for ct in range(pieces):
                cols = slice(ct * lanes, (ct + 1) * lanes)
                tile = recv_ref[ct, start : start + depth, :].astype(jnp.float32)
                value = noise_ref[:, cols] * tile
                if part == 0:
                    hit = base + ct * lanes == spot_at
                    value = value + jnp.where(hit, point_size, 0.0)
                lo_ref[b, part, :, cols] = value[:half]
                hi_ref[b, part, :, cols] = value[half:]


def sweep_kernel(depth, meta_ref, lo_ref, hi_ref, below_ref, above_ref, wave_ref, wbelow_ref,
                 wabove_ref, out_ref, are_ref, aim_ref, bre_ref, bim_ref, sre_ref, sim_ref, w_ref,
                 sr_ref, si_ref):
    half = depth // 2
    rows, cells = sre_ref.shape
    width = LANES
    chunks = cells // width
    slab = meta_ref[0]
    nslab = meta_ref[1]
    w_ref[0:HALO] = wbelow_ref[...]
    w_ref[HALO : HALO + depth] = wave_ref[...]
    w_ref[HALO + depth :] = wabove_ref[...]
    for part, dst in ((0, sre_ref), (1, sim_ref)):
        dst[0:HALO] = below_ref[0, part]
        dst[HALO : HALO + half] = lo_ref[0, part]
        dst[HALO + half : HALO + depth] = hi_ref[0, part]
        dst[HALO + depth :] = above_ref[0, part]
    zeros = jnp.zeros((rows, PAD), jnp.float32)
    for ref in (are_ref, aim_ref, bre_ref, bim_ref):
        ref[:, 0:PAD] = zeros
        ref[:, PAD + cells :] = zeros
    row = lax.broadcasted_iota(jnp.int32, (rows, width), 0)
    inside = jnp.logical_and(
        jnp.logical_or(row >= HALO, slab > 0),
        jnp.logical_or(row < HALO + depth, slab < nslab - 1),
    )

    def first(j, carry):
        c0 = pl.multiple_of(j * width, width)
        cols = pl.ds(c0, width)
        wave = w_ref[:, cols]
        diag_real = 6.0 - wave
        denom = diag_real * diag_real + damping * wave * (damping * wave)
        sr = jnp.where(inside, relaxation * diag_real / denom, 0.0)
        si = jnp.where(inside, relaxation * damping * wave / denom, 0.0)
        sr_ref[:, cols] = sr
        si_ref[:, cols] = si
        src_re = sre_ref[:, cols]
        src_im = sim_ref[:, cols]
        out = pl.ds(PAD + c0, width)
        are_ref[:, out] = sr * src_re - si * src_im
        aim_ref[:, out] = sr * src_im + si * src_re
        return carry

    lax.fori_loop(0, chunks, first, 0)

    keep = 1.0 - relaxation
    lane = lax.broadcasted_iota(jnp.int32, (rows, width), 1)
    col = jnp.bitwise_and(lane, GY - 1)
    has_ym = col != 0
    has_yp = col != GY - 1

    def sweep(src_pair, dst_pair, last):
        def chunk(j, carry):
            c0 = pl.multiple_of(j * width, width)
            cols = pl.ds(c0, width)

            def total(ref, src):
                ext = ref[:, pl.ds(c0, width + 2 * PAD)]
                rot = pltpu.roll(ext, GY, 1)
                mid = ext[:, PAD : PAD + width]
                xm = rot[:, PAD : PAD + width]
                xp = rot[:, 2 * PAD : 2 * PAD + width]
                ym = jnp.where(has_ym, pltpu.roll(mid, 1, 1), 0.0)
                yp = jnp.where(has_yp, pltpu.roll(mid, width - 1, 1), 0.0)
                dn = pltpu.roll(mid, 1, 0)
                up = pltpu.roll(mid, rows - 1, 0)
                return mid, src + (xm + xp + ym + yp + dn + up)

            re, t_re = total(src_pair[0], sre_ref[:, cols])
            im, t_im = total(src_pair[1], sim_ref[:, cols])
            s_r = sr_ref[:, cols]
            s_i = si_ref[:, cols]
            new_re = keep * re + (s_r * t_re - s_i * t_im)
            new_im = keep * im + (s_r * t_im + s_i * t_re)
            if last:
                out_ref[0, 0, :, cols] = new_re[HALO : HALO + depth]
                out_ref[1, 0, :, cols] = new_im[HALO : HALO + depth]
            else:
                dst_pair[0][:, pl.ds(PAD + c0, width)] = new_re
                dst_pair[1][:, pl.ds(PAD + c0, width)] = new_im
            return carry

        lax.fori_loop(0, chunks, chunk, 0, unroll=True)

    pairs = ((are_ref, aim_ref), (bre_ref, bim_ref))
    for k in range(SWEEPS - 1):
        sweep(pairs[k % 2], pairs[(k + 1) % 2], k == SWEEPS - 2)


def sweeps(meta, lo, hi, below, above, wave, wbelow, wabove):
    owned, _, half, cells = lo.shape
    depth = 2 * half
    rows = depth + 2 * HALO
    piece = pl.BlockSpec((1, 2, half, cells), lambda b, *_: (b, 0, 0, 0))
    halo = pl.BlockSpec((1, 2, HALO, cells), lambda b, *_: (b, 0, 0, 0))
    whole = lambda shape: pl.BlockSpec(shape, lambda b, *_: (0,) * len(shape))
    grid_spec = pltpu.PrefetchScalarGridSpec(
        num_scalar_prefetch=1,
        grid=(owned,),
        in_specs=[piece, piece, halo, halo, whole((depth, cells)), whole((HALO, cells)),
                  whole((HALO, cells))],
        out_specs=pl.BlockSpec((2, 1, depth, cells), lambda b, *_: (0, b, 0, 0)),
        scratch_shapes=[pltpu.VMEM((rows, cells + 2 * PAD), jnp.float32) for _ in range(4)]
        + [pltpu.VMEM((rows, cells), jnp.float32) for _ in range(5)],
    )
    return pl.pallas_call(
        functools.partial(sweep_kernel, depth),
        out_shape=jax.ShapeDtypeStruct((2, owned, depth, cells), jnp.float32),
        grid_spec=grid_spec,
        cost_estimate=pl.CostEstimate(
            flops=owned * SWEEPS * 60 * rows * cells,
            bytes_accessed=owned * 4 * cells * (6 * depth),
            transcendentals=0,
        ),
    )(meta, lo, hi, below, above, wave, wbelow, wabove)


def local(green_fields, pair_list, pair_values, noise_map, wave_square, station_cell):
    parts, owned, depth, cells = green_fields.shape
    nsta = lax.axis_size("sta")
    nslab = lax.axis_size("slab")
    count = owned * nsta
    lanes = cells // nsta
    slab = lax.axis_index("slab")
    up_pairs = [(i, i + 1) for i in range(nslab - 1)]
    down_pairs = [(i + 1, i) for i in range(nslab - 1)]
    half = depth // 2

    send = green_fields.reshape(parts, owned, depth, nsta, lanes)
    send = send.transpose(3, 0, 1, 2, 4).reshape(nsta, parts * owned * depth, lanes)
    recv = lax.all_to_all(send, "sta", 0, 0, tiled=True)

    big = build_resid(pair_list, pair_values, count)
    size = 2 * count
    new = jnp.arange(size, dtype=jnp.int32)
    old_row = (new % 2) * count + new // 2
    src, rest = new // (2 * owned), new % (2 * owned)
    old_col = (rest // owned) * count + src * owned + rest % owned
    pick_rows = (old_row[:, None] == new[None, :]).astype(jnp.bfloat16)
    pick_cols = (new[:, None] == old_col[None, :]).astype(jnp.bfloat16)
    big = jnp.dot(pick_rows, big, preferred_element_type=jnp.float32).astype(jnp.bfloat16)
    big = jnp.dot(big, pick_cols, preferred_element_type=jnp.float32).astype(jnp.bfloat16)
    big, wave_hi, wave_lo = lax.optimization_barrier(
        (big, wave_square[depth - HALO :], wave_square[:HALO])
    )
    wbelow = lax.ppermute(wave_hi, "slab", up_pairs)
    wabove = lax.ppermute(wave_lo, "slab", down_pairs)
    big, wbelow, wabove = lax.optimization_barrier((big, wbelow, wabove))
    mixed = mix(big, recv.reshape(nsta * parts * owned * depth, lanes), depth)
    back = lax.all_to_all(mixed.reshape(nsta, owned * parts * depth, lanes), "sta", 0, 0,
                          tiled=True)

    meta = jnp.concatenate(
        [jnp.stack([slab, jnp.int32(nslab)]).astype(jnp.int32), station_cell.astype(jnp.int32)]
    )
    lo, hi = pl.pallas_call(
        functools.partial(source_kernel, owned, depth),
        out_shape=[jax.ShapeDtypeStruct((owned, 2, half, cells), jnp.float32)] * 2,
        in_specs=[
            pl.BlockSpec(memory_space=pltpu.SMEM),
            pl.BlockSpec(memory_space=pltpu.VMEM),
            pl.BlockSpec(memory_space=pltpu.VMEM),
        ],
    )(meta, back, noise_map)
    below = lax.ppermute(hi, "slab", up_pairs)
    above = lax.ppermute(lo, "slab", down_pairs)
    return sweeps(meta, lo, hi, below, above, wave_square, wbelow, wabove)


def solution(mesh):
    placed = (P(None, "sta", "slab", None), P(), P(), P("slab", None), P("slab", None), P("sta"))
    return jax.shard_map(
        local, mesh=mesh, in_specs=placed, out_specs=P(None, "sta", "slab", None), check_vma=False
    )
```

```python
import functools

import jax
import jax.numpy as jnp
from jax import lax
from jax.experimental import pallas as pl
from jax.experimental.pallas import tpu as pltpu
from jax.sharding import PartitionSpec as P

GY = 64
SWEEPS = 6
HALO = 8
LANES = 512
PAD = 128

damping = 0.3
relaxation = 0.8
point_size = 2.0


def build_resid(pair_list, pair_values, count):
    labels = jnp.arange(count, dtype=jnp.int32)
    first = (pair_list[:, 0:1] == labels[None, :]).astype(jnp.float32)
    second = (pair_list[:, 1:2] == labels[None, :]).astype(jnp.float32)
    real_w = pair_values[0][:, None]
    imag_w = pair_values[1][:, None]
    highest = lax.Precision.HIGHEST
    resid_real = jnp.dot(
        first.T, real_w * second, precision=highest, preferred_element_type=jnp.float32
    ) + jnp.dot(second.T, real_w * first, precision=highest, preferred_element_type=jnp.float32)
    resid_imag = jnp.dot(
        first.T, imag_w * second, precision=highest, preferred_element_type=jnp.float32
    ) - jnp.dot(second.T, imag_w * first, precision=highest, preferred_element_type=jnp.float32)
    resid_real = resid_real.astype(jnp.bfloat16)
    resid_imag = resid_imag.astype(jnp.bfloat16)
    upper = jnp.concatenate([resid_real, -resid_imag], axis=1)
    lower = jnp.concatenate([resid_imag, resid_real], axis=1)
    return jnp.concatenate([upper, lower], axis=0)


def pack_kernel(green_ref, send_ref):
    parts, owned, depth, cells = green_ref.shape
    pieces, _, lanes = send_ref.shape
    for part in range(parts):
        for b in range(owned):
            start = (part * owned + b) * depth
            for ct in range(pieces):
                send_ref[ct, start : start + depth, :] = green_ref[part, b, :, ct * lanes : (ct + 1) * lanes]


def mix_kernel(depth, big_ref, recv_ref, out_ref, wide_ref, acc_ref):
    wide_ref[...] = recv_ref[...].astype(jnp.float32)
    big = big_ref[...]
    rows = big.shape[0]
    for r in range(depth):
        rhs = wide_ref[pl.ds(r, rows, stride=depth), :].astype(jnp.bfloat16)
        acc_ref[pl.ds(r, rows, stride=depth), :] = jnp.dot(
            big, rhs, preferred_element_type=jnp.float32
        )
    out_ref[...] = acc_ref[...].astype(out_ref.dtype)


def mix(big, recv, depth):
    total, lanes = recv.shape
    return pl.pallas_call(
        functools.partial(mix_kernel, depth),
        out_shape=jax.ShapeDtypeStruct((total, lanes), jnp.bfloat16),
        scratch_shapes=[
            pltpu.VMEM((total, lanes), jnp.float32),
            pltpu.VMEM((total, lanes), jnp.float32),
        ],
        cost_estimate=pl.CostEstimate(
            flops=2 * big.shape[0] * big.shape[1] * depth * lanes,
            bytes_accessed=4 * total * lanes,
            transcendentals=0,
        ),
    )(big, recv)


def source_kernel(owned, depth, meta_ref, recv_ref, noise_ref, lo_ref, hi_ref):
    pieces, _, lanes = recv_ref.shape
    half = depth // 2
    slab = meta_ref[0]
    row = lax.broadcasted_iota(jnp.int32, (depth, lanes), 0)
    lane = lax.broadcasted_iota(jnp.int32, (depth, lanes), 1)
    base = (slab * depth + row) * (pieces * lanes) + lane
    for b in range(owned):
        spot_at = meta_ref[2 + b]
        for part in range(2):
            start = (b * 2 + part) * depth
            for ct in range(pieces):
                cols = slice(ct * lanes, (ct + 1) * lanes)
                tile = recv_ref[ct, start : start + depth, :].astype(jnp.float32)
                value = noise_ref[:, cols] * tile
                if part == 0:
                    hit = base + ct * lanes == spot_at
                    value = value + jnp.where(hit, point_size, 0.0)
                lo_ref[b, part, :, cols] = value[:half]
                hi_ref[b, part, :, cols] = value[half:]


def sweep_kernel(depth, meta_ref, lo_ref, hi_ref, below_ref, above_ref, wave_ref, wbelow_ref,
                 wabove_ref, out_ref, are_ref, aim_ref, bre_ref, bim_ref, sre_ref, sim_ref, w_ref,
                 sr_ref, si_ref):
    half = depth // 2
    rows, cells = sre_ref.shape
    width = LANES
    chunks = cells // width
    slab = meta_ref[0]
    nslab = meta_ref[1]
    w_ref[0:HALO] = wbelow_ref[...]
    w_ref[HALO : HALO + depth] = wave_ref[...]
    w_ref[HALO + depth :] = wabove_ref[...]
    for part, dst in ((0, sre_ref), (1, sim_ref)):
        dst[0:HALO] = below_ref[0, part]
        dst[HALO : HALO + half] = lo_ref[0, part]
        dst[HALO + half : HALO + depth] = hi_ref[0, part]
        dst[HALO + depth :] = above_ref[0, part]
    zeros = jnp.zeros((rows, PAD), jnp.float32)
    for ref in (are_ref, aim_ref, bre_ref, bim_ref):
        ref[:, 0:PAD] = zeros
        ref[:, PAD + cells :] = zeros
    row = lax.broadcasted_iota(jnp.int32, (rows, width), 0)
    inside = jnp.logical_and(
        jnp.logical_or(row >= HALO, slab > 0),
        jnp.logical_or(row < HALO + depth, slab < nslab - 1),
    )

    def first(j, carry):
        c0 = pl.multiple_of(j * width, width)
        cols = pl.ds(c0, width)
        wave = w_ref[:, cols]
        diag_real = 6.0 - wave
        denom = diag_real * diag_real + damping * wave * (damping * wave)
        sr = jnp.where(inside, relaxation * diag_real / denom, 0.0)
        si = jnp.where(inside, relaxation * damping * wave / denom, 0.0)
        sr_ref[:, cols] = sr
        si_ref[:, cols] = si
        src_re = sre_ref[:, cols]
        src_im = sim_ref[:, cols]
        out = pl.ds(PAD + c0, width)
        are_ref[:, out] = sr * src_re - si * src_im
        aim_ref[:, out] = sr * src_im + si * src_re
        return carry

    lax.fori_loop(0, chunks, first, 0)

    keep = 1.0 - relaxation
    lane = lax.broadcasted_iota(jnp.int32, (rows, width), 1)
    col = jnp.bitwise_and(lane, GY - 1)
    has_ym = col != 0
    has_yp = col != GY - 1

    def sweep(src_pair, dst_pair, last):
        def chunk(j, carry):
            c0 = pl.multiple_of(j * width, width)
            cols = pl.ds(c0, width)

            def total(ref, src):
                ext = ref[:, pl.ds(c0, width + 2 * PAD)]
                rot = pltpu.roll(ext, GY, 1)
                mid = ext[:, PAD : PAD + width]
                xm = rot[:, PAD : PAD + width]
                xp = rot[:, 2 * PAD : 2 * PAD + width]
                ym = jnp.where(has_ym, pltpu.roll(mid, 1, 1), 0.0)
                yp = jnp.where(has_yp, pltpu.roll(mid, width - 1, 1), 0.0)
                dn = pltpu.roll(mid, 1, 0)
                up = pltpu.roll(mid, rows - 1, 0)
                return mid, src + (xm + xp + ym + yp + dn + up)

            re, t_re = total(src_pair[0], sre_ref[:, cols])
            im, t_im = total(src_pair[1], sim_ref[:, cols])
            s_r = sr_ref[:, cols]
            s_i = si_ref[:, cols]
            new_re = keep * re + (s_r * t_re - s_i * t_im)
            new_im = keep * im + (s_r * t_im + s_i * t_re)
            if last:
                out_ref[0, 0, :, cols] = new_re[HALO : HALO + depth]
                out_ref[1, 0, :, cols] = new_im[HALO : HALO + depth]
            else:
                dst_pair[0][:, pl.ds(PAD + c0, width)] = new_re
                dst_pair[1][:, pl.ds(PAD + c0, width)] = new_im
            return carry

        lax.fori_loop(0, chunks, chunk, 0, unroll=True)

    pairs = ((are_ref, aim_ref), (bre_ref, bim_ref))
    for k in range(SWEEPS - 1):
        sweep(pairs[k % 2], pairs[(k + 1) % 2], k == SWEEPS - 2)


def sweeps(meta, lo, hi, below, above, wave, wbelow, wabove):
    owned, _, half, cells = lo.shape
    depth = 2 * half
    rows = depth + 2 * HALO
    piece = pl.BlockSpec((1, 2, half, cells), lambda b, *_: (b, 0, 0, 0))
    halo = pl.BlockSpec((1, 2, HALO, cells), lambda b, *_: (b, 0, 0, 0))
    whole = lambda shape: pl.BlockSpec(shape, lambda b, *_: (0,) * len(shape))
    grid_spec = pltpu.PrefetchScalarGridSpec(
        num_scalar_prefetch=1,
        grid=(owned,),
        in_specs=[piece, piece, halo, halo, whole((depth, cells)), whole((HALO, cells)),
                  whole((HALO, cells))],
        out_specs=pl.BlockSpec((2, 1, depth, cells), lambda b, *_: (0, b, 0, 0)),
        scratch_shapes=[pltpu.VMEM((rows, cells + 2 * PAD), jnp.float32) for _ in range(4)]
        + [pltpu.VMEM((rows, cells), jnp.float32) for _ in range(5)],
    )
    return pl.pallas_call(
        functools.partial(sweep_kernel, depth),
        out_shape=jax.ShapeDtypeStruct((2, owned, depth, cells), jnp.float32),
        grid_spec=grid_spec,
        cost_estimate=pl.CostEstimate(
            flops=owned * SWEEPS * 60 * rows * cells,
            bytes_accessed=owned * 4 * cells * (6 * depth),
            transcendentals=0,
        ),
    )(meta, lo, hi, below, above, wave, wbelow, wabove)


def local(green_fields, pair_list, pair_values, noise_map, wave_square, station_cell):
    parts, owned, depth, cells = green_fields.shape
    nsta = lax.axis_size("sta")
    nslab = lax.axis_size("slab")
    count = owned * nsta
    lanes = cells // nsta
    slab = lax.axis_index("slab")
    up_pairs = [(i, i + 1) for i in range(nslab - 1)]
    down_pairs = [(i + 1, i) for i in range(nslab - 1)]
    half = depth // 2

    send = pl.pallas_call(
        pack_kernel,
        out_shape=jax.ShapeDtypeStruct((nsta, parts * owned * depth, lanes), green_fields.dtype),
    )(green_fields)
    recv = lax.all_to_all(send, "sta", 0, 0, tiled=True)

    big = build_resid(pair_list, pair_values, count)
    size = 2 * count
    new = jnp.arange(size, dtype=jnp.int32)
    old_row = (new % 2) * count + new // 2
    src, rest = new // (2 * owned), new % (2 * owned)
    old_col = (rest // owned) * count + src * owned + rest % owned
    pick_rows = (old_row[:, None] == new[None, :]).astype(jnp.bfloat16)
    pick_cols = (new[:, None] == old_col[None, :]).astype(jnp.bfloat16)
    big = jnp.dot(pick_rows, big, preferred_element_type=jnp.float32).astype(jnp.bfloat16)
    big = jnp.dot(big, pick_cols, preferred_element_type=jnp.float32).astype(jnp.bfloat16)
    big, wave_hi, wave_lo = lax.optimization_barrier(
        (big, wave_square[depth - HALO :], wave_square[:HALO])
    )
    wbelow = lax.ppermute(wave_hi, "slab", up_pairs)
    wabove = lax.ppermute(wave_lo, "slab", down_pairs)
    big, wbelow, wabove = lax.optimization_barrier((big, wbelow, wabove))
    mixed = mix(big, recv.reshape(nsta * parts * owned * depth, lanes), depth)
    back = lax.all_to_all(mixed.reshape(nsta, owned * parts * depth, lanes), "sta", 0, 0,
                          tiled=True)

    meta = jnp.concatenate(
        [jnp.stack([slab, jnp.int32(nslab)]).astype(jnp.int32), station_cell.astype(jnp.int32)]
    )
    lo, hi = pl.pallas_call(
        functools.partial(source_kernel, owned, depth),
        out_shape=[jax.ShapeDtypeStruct((owned, 2, half, cells), jnp.float32)] * 2,
        in_specs=[
            pl.BlockSpec(memory_space=pltpu.SMEM),
            pl.BlockSpec(memory_space=pltpu.VMEM),
            pl.BlockSpec(memory_space=pltpu.VMEM),
        ],
    )(meta, back, noise_map)
    below = lax.ppermute(hi, "slab", up_pairs)
    above = lax.ppermute(lo, "slab", down_pairs)
    return sweeps(meta, lo, hi, below, above, wave_square, wbelow, wabove)


def solution(mesh):
    placed = (P(None, "sta", "slab", None), P(), P(), P("slab", None), P("slab", None), P("sta"))
    return jax.shard_map(
        local, mesh=mesh, in_specs=placed, out_specs=P(None, "sta", "slab", None), check_vma=False
    )
```

```python
import functools

import jax
import jax.numpy as jnp
from jax import lax
from jax.experimental import pallas as pl
from jax.experimental.pallas import tpu as pltpu
from jax.sharding import PartitionSpec as P

GY = 64
SWEEPS = 6
HALO = 8
LANES = 512
PAD = 128

damping = 0.3
relaxation = 0.8
point_size = 2.0


def build_resid(pair_list, pair_values, count):
    labels = jnp.arange(count, dtype=jnp.int32)
    first = (pair_list[:, 0:1] == labels[None, :]).astype(jnp.float32)
    second = (pair_list[:, 1:2] == labels[None, :]).astype(jnp.float32)
    real_w = pair_values[0][:, None]
    imag_w = pair_values[1][:, None]
    highest = lax.Precision.HIGHEST
    resid_real = jnp.dot(
        first.T, real_w * second, precision=highest, preferred_element_type=jnp.float32
    ) + jnp.dot(second.T, real_w * first, precision=highest, preferred_element_type=jnp.float32)
    resid_imag = jnp.dot(
        first.T, imag_w * second, precision=highest, preferred_element_type=jnp.float32
    ) - jnp.dot(second.T, imag_w * first, precision=highest, preferred_element_type=jnp.float32)
    resid_real = resid_real.astype(jnp.bfloat16)
    resid_imag = resid_imag.astype(jnp.bfloat16)
    upper = jnp.concatenate([resid_real, -resid_imag], axis=1)
    lower = jnp.concatenate([resid_imag, resid_real], axis=1)
    return jnp.concatenate([upper, lower], axis=0)


def pack_kernel(green_ref, send_ref):
    parts, owned, depth, cells = green_ref.shape
    pieces, _, lanes = send_ref.shape
    for part in range(parts):
        for b in range(owned):
            start = (part * owned + b) * depth
            for ct in range(pieces):
                send_ref[ct, start : start + depth, :] = green_ref[part, b, :, ct * lanes : (ct + 1) * lanes]


def mix_kernel(depth, big_ref, recv_ref, out_ref, wide_ref, acc_ref):
    wide_ref[...] = recv_ref[...].astype(jnp.float32)
    big = big_ref[...]
    rows = big.shape[0]
    for r in range(depth):
        rhs = wide_ref[pl.ds(r, rows, stride=depth), :].astype(jnp.bfloat16)
        acc_ref[pl.ds(r, rows, stride=depth), :] = jnp.dot(
            big, rhs, preferred_element_type=jnp.float32
        )
    out_ref[...] = acc_ref[...].astype(out_ref.dtype)


def mix(big, recv, depth):
    total, lanes = recv.shape
    return pl.pallas_call(
        functools.partial(mix_kernel, depth),
        out_shape=jax.ShapeDtypeStruct((total, lanes), jnp.bfloat16),
        scratch_shapes=[
            pltpu.VMEM((total, lanes), jnp.float32),
            pltpu.VMEM((total, lanes), jnp.float32),
        ],
        cost_estimate=pl.CostEstimate(
            flops=2 * big.shape[0] * big.shape[1] * depth * lanes,
            bytes_accessed=4 * total * lanes,
            transcendentals=0,
        ),
    )(big, recv)


def source_kernel(owned, depth, meta_ref, recv_ref, noise_ref, lo_ref, hi_ref):
    pieces, _, lanes = recv_ref.shape
    half = depth // 2
    slab = meta_ref[0]
    row = lax.broadcasted_iota(jnp.int32, (depth, lanes), 0)
    lane = lax.broadcasted_iota(jnp.int32, (depth, lanes), 1)
    base = (slab * depth + row) * (pieces * lanes) + lane
    for b in range(owned):
        spot_at = meta_ref[2 + b]
        for part in range(2):
            start = (b * 2 + part) * depth
            for ct in range(pieces):
                cols = slice(ct * lanes, (ct + 1) * lanes)
                tile = recv_ref[ct, start : start + depth, :].astype(jnp.float32)
                value = noise_ref[:, cols] * tile
                if part == 0:
                    hit = base + ct * lanes == spot_at
                    value = value + jnp.where(hit, point_size, 0.0)
                lo_ref[b, part, :, cols] = value[:half]
                hi_ref[b, part, :, cols] = value[half:]


def sweep_kernel(depth, meta_ref, lo_ref, hi_ref, below_ref, above_ref, wave_ref, wbelow_ref,
                 wabove_ref, out_ref, are_ref, aim_ref, bre_ref, bim_ref, sre_ref, sim_ref, w_ref,
                 sr_ref, si_ref):
    half = depth // 2
    rows, cells = sre_ref.shape
    width = LANES
    chunks = cells // width
    slab = meta_ref[0]
    nslab = meta_ref[1]
    w_ref[0:HALO] = wbelow_ref[...]
    w_ref[HALO : HALO + depth] = wave_ref[...]
    w_ref[HALO + depth :] = wabove_ref[...]
    for part, dst in ((0, sre_ref), (1, sim_ref)):
        dst[0:HALO] = below_ref[0, part]
        dst[HALO : HALO + half] = lo_ref[0, part]
        dst[HALO + half : HALO + depth] = hi_ref[0, part]
        dst[HALO + depth :] = above_ref[0, part]
    zeros = jnp.zeros((rows, PAD), jnp.float32)
    for ref in (are_ref, aim_ref, bre_ref, bim_ref):
        ref[:, 0:PAD] = zeros
        ref[:, PAD + cells :] = zeros
    row = lax.broadcasted_iota(jnp.int32, (rows, width), 0)
    inside = jnp.logical_and(
        jnp.logical_or(row >= HALO, slab > 0),
        jnp.logical_or(row < HALO + depth, slab < nslab - 1),
    )

    def first(j, carry):
        c0 = pl.multiple_of(j * width, width)
        cols = pl.ds(c0, width)
        wave = w_ref[:, cols]
        diag_real = 6.0 - wave
        denom = diag_real * diag_real + damping * wave * (damping * wave)
        sr = jnp.where(inside, relaxation * diag_real / denom, 0.0)
        si = jnp.where(inside, relaxation * damping * wave / denom, 0.0)
        sr_ref[:, cols] = sr
        si_ref[:, cols] = si
        src_re = sre_ref[:, cols]
        src_im = sim_ref[:, cols]
        out = pl.ds(PAD + c0, width)
        are_ref[:, out] = sr * src_re - si * src_im
        aim_ref[:, out] = sr * src_im + si * src_re
        return carry

    lax.fori_loop(0, chunks, first, 0)

    keep = 1.0 - relaxation
    lane = lax.broadcasted_iota(jnp.int32, (rows, width), 1)
    col = jnp.bitwise_and(lane, GY - 1)
    has_ym = col != 0
    has_yp = col != GY - 1

    def sweep(src_pair, dst_pair, last):
        def chunk(j, carry):
            c0 = pl.multiple_of(j * width, width)
            cols = pl.ds(c0, width)

            def total(ref, src):
                ext = ref[:, pl.ds(c0, width + 2 * PAD)]
                rot = pltpu.roll(ext, GY, 1)
                mid = ext[:, PAD : PAD + width]
                xm = rot[:, PAD : PAD + width]
                xp = rot[:, 2 * PAD : 2 * PAD + width]
                ym = jnp.where(has_ym, pltpu.roll(mid, 1, 1), 0.0)
                yp = jnp.where(has_yp, pltpu.roll(mid, width - 1, 1), 0.0)
                dn = pltpu.roll(mid, 1, 0)
                up = pltpu.roll(mid, rows - 1, 0)
                return mid, src + (xm + xp + ym + yp + dn + up)

            re, t_re = total(src_pair[0], sre_ref[:, cols])
            im, t_im = total(src_pair[1], sim_ref[:, cols])
            s_r = sr_ref[:, cols]
            s_i = si_ref[:, cols]
            new_re = keep * re + (s_r * t_re - s_i * t_im)
            new_im = keep * im + (s_r * t_im + s_i * t_re)
            if last:
                out_ref[0, 0, :, cols] = new_re[HALO : HALO + depth]
                out_ref[1, 0, :, cols] = new_im[HALO : HALO + depth]
            else:
                dst_pair[0][:, pl.ds(PAD + c0, width)] = new_re
                dst_pair[1][:, pl.ds(PAD + c0, width)] = new_im
            return carry

        lax.fori_loop(0, chunks, chunk, 0, unroll=True)

    pairs = ((are_ref, aim_ref), (bre_ref, bim_ref))
    for k in range(SWEEPS - 1):
        sweep(pairs[k % 2], pairs[(k + 1) % 2], k == SWEEPS - 2)


def sweeps(meta, lo, hi, below, above, wave, wbelow, wabove):
    owned, _, half, cells = lo.shape
    depth = 2 * half
    rows = depth + 2 * HALO
    piece = pl.BlockSpec((1, 2, half, cells), lambda b, *_: (b, 0, 0, 0))
    halo = pl.BlockSpec((1, 2, HALO, cells), lambda b, *_: (b, 0, 0, 0))
    whole = lambda shape: pl.BlockSpec(shape, lambda b, *_: (0,) * len(shape))
    grid_spec = pltpu.PrefetchScalarGridSpec(
        num_scalar_prefetch=1,
        grid=(owned,),
        in_specs=[piece, piece, halo, halo, whole((depth, cells)), whole((HALO, cells)),
                  whole((HALO, cells))],
        out_specs=pl.BlockSpec((2, 1, depth, cells), lambda b, *_: (0, b, 0, 0)),
        scratch_shapes=[pltpu.VMEM((rows, cells + 2 * PAD), jnp.float32) for _ in range(4)]
        + [pltpu.VMEM((rows, cells), jnp.float32) for _ in range(5)],
    )
    return pl.pallas_call(
        functools.partial(sweep_kernel, depth),
        out_shape=jax.ShapeDtypeStruct((2, owned, depth, cells), jnp.float32),
        grid_spec=grid_spec,
        cost_estimate=pl.CostEstimate(
            flops=owned * SWEEPS * 60 * rows * cells,
            bytes_accessed=owned * 4 * cells * (6 * depth),
            transcendentals=0,
        ),
    )(meta, lo, hi, below, above, wave, wbelow, wabove)


def local(green_fields, pair_list, pair_values, noise_map, wave_square, station_cell):
    parts, owned, depth, cells = green_fields.shape
    nsta = lax.axis_size("sta")
    nslab = lax.axis_size("slab")
    count = owned * nsta
    lanes = cells // nsta
    slab = lax.axis_index("slab")
    up_pairs = [(i, i + 1) for i in range(nslab - 1)]
    down_pairs = [(i + 1, i) for i in range(nslab - 1)]
    half = depth // 2

    send = pl.pallas_call(
        pack_kernel,
        out_shape=jax.ShapeDtypeStruct((nsta, parts * owned * depth, lanes), green_fields.dtype),
    )(green_fields)
    recv = lax.all_to_all(send, "sta", 0, 0, tiled=True)

    big = build_resid(pair_list, pair_values, count)
    size = 2 * count
    new = jnp.arange(size, dtype=jnp.int32)
    old_row = (new % 2) * count + new // 2
    src, rest = new // (2 * owned), new % (2 * owned)
    old_col = (rest // owned) * count + src * owned + rest % owned
    pick_rows = (old_row[:, None] == new[None, :]).astype(jnp.bfloat16)
    pick_cols = (new[:, None] == old_col[None, :]).astype(jnp.bfloat16)
    big = jnp.dot(pick_rows, big, preferred_element_type=jnp.float32).astype(jnp.bfloat16)
    big = jnp.dot(big, pick_cols, preferred_element_type=jnp.float32).astype(jnp.bfloat16)
    big, wave_hi, wave_lo = lax.optimization_barrier(
        (big, wave_square[depth - HALO :], wave_square[:HALO])
    )
    wbelow = lax.ppermute(wave_hi, "slab", up_pairs)
    wabove = lax.ppermute(wave_lo, "slab", down_pairs)
    mixed = mix(big, recv.reshape(nsta * parts * owned * depth, lanes), depth)
    back = lax.all_to_all(mixed.reshape(nsta, owned * parts * depth, lanes), "sta", 0, 0,
                          tiled=True)
    back, wbelow, wabove = lax.optimization_barrier((back, wbelow, wabove))

    meta = jnp.concatenate(
        [jnp.stack([slab, jnp.int32(nslab)]).astype(jnp.int32), station_cell.astype(jnp.int32)]
    )
    lo, hi = pl.pallas_call(
        functools.partial(source_kernel, owned, depth),
        out_shape=[jax.ShapeDtypeStruct((owned, 2, half, cells), jnp.float32)] * 2,
        in_specs=[
            pl.BlockSpec(memory_space=pltpu.SMEM),
            pl.BlockSpec(memory_space=pltpu.VMEM),
            pl.BlockSpec(memory_space=pltpu.VMEM),
        ],
    )(meta, back, noise_map)
    below = lax.ppermute(hi, "slab", up_pairs)
    above = lax.ppermute(lo, "slab", down_pairs)
    return sweeps(meta, lo, hi, below, above, wave_square, wbelow, wabove)


def solution(mesh):
    placed = (P(None, "sta", "slab", None), P(), P(), P("slab", None), P("slab", None), P("sta"))
    return jax.shard_map(
        local, mesh=mesh, in_specs=placed, out_specs=P(None, "sta", "slab", None), check_vma=False
    )
```

```python
import functools

import jax
import jax.numpy as jnp
from jax import lax
from jax.experimental import pallas as pl
from jax.experimental.pallas import tpu as pltpu
from jax.sharding import PartitionSpec as P

GY = 64
SWEEPS = 6
HALO = 8
LANES = 512
PAD = 128

damping = 0.3
relaxation = 0.8
point_size = 2.0


def build_resid(pair_list, pair_values, count):
    labels = jnp.arange(count, dtype=jnp.int32)
    first = (pair_list[:, 0:1] == labels[None, :]).astype(jnp.float32)
    second = (pair_list[:, 1:2] == labels[None, :]).astype(jnp.float32)
    real_w = pair_values[0][:, None]
    imag_w = pair_values[1][:, None]
    highest = lax.Precision.HIGHEST
    resid_real = jnp.dot(
        first.T, real_w * second, precision=highest, preferred_element_type=jnp.float32
    ) + jnp.dot(second.T, real_w * first, precision=highest, preferred_element_type=jnp.float32)
    resid_imag = jnp.dot(
        first.T, imag_w * second, precision=highest, preferred_element_type=jnp.float32
    ) - jnp.dot(second.T, imag_w * first, precision=highest, preferred_element_type=jnp.float32)
    resid_real = resid_real.astype(jnp.bfloat16)
    resid_imag = resid_imag.astype(jnp.bfloat16)
    upper = jnp.concatenate([resid_real, -resid_imag], axis=1)
    lower = jnp.concatenate([resid_imag, resid_real], axis=1)
    return jnp.concatenate([upper, lower], axis=0)


def pack_kernel(green_ref, send_ref):
    parts, owned, depth, cells = green_ref.shape
    pieces, _, lanes = send_ref.shape
    for part in range(parts):
        for b in range(owned):
            start = (part * owned + b) * depth
            for ct in range(pieces):
                send_ref[ct, start : start + depth, :] = green_ref[part, b, :, ct * lanes : (ct + 1) * lanes]


def mix_kernel(depth, big_ref, recv_ref, out_ref, wide_ref, acc_ref):
    wide_ref[...] = recv_ref[...].astype(jnp.float32)
    big = big_ref[...]
    rows = big.shape[0]
    for r in range(depth):
        rhs = wide_ref[pl.ds(r, rows, stride=depth), :].astype(jnp.bfloat16)
        acc_ref[pl.ds(r, rows, stride=depth), :] = jnp.dot(
            big, rhs, preferred_element_type=jnp.float32
        )
    out_ref[...] = acc_ref[...].astype(out_ref.dtype)


def mix(big, recv, depth):
    total, lanes = recv.shape
    return pl.pallas_call(
        functools.partial(mix_kernel, depth),
        out_shape=jax.ShapeDtypeStruct((total, lanes), jnp.bfloat16),
        scratch_shapes=[
            pltpu.VMEM((total, lanes), jnp.float32),
            pltpu.VMEM((total, lanes), jnp.float32),
        ],
        cost_estimate=pl.CostEstimate(
            flops=2 * big.shape[0] * big.shape[1] * depth * lanes,
            bytes_accessed=4 * total * lanes,
            transcendentals=0,
        ),
    )(big, recv)


def source_kernel(owned, depth, meta_ref, recv_ref, noise_ref, lo_ref, hi_ref):
    pieces, _, lanes = recv_ref.shape
    half = depth // 2
    slab = meta_ref[0]
    row = lax.broadcasted_iota(jnp.int32, (depth, lanes), 0)
    lane = lax.broadcasted_iota(jnp.int32, (depth, lanes), 1)
    base = (slab * depth + row) * (pieces * lanes) + lane
    for b in range(owned):
        spot_at = meta_ref[2 + b]
        for part in range(2):
            start = (b * 2 + part) * depth
            for ct in range(pieces):
                cols = slice(ct * lanes, (ct + 1) * lanes)
                tile = recv_ref[ct, start : start + depth, :].astype(jnp.float32)
                value = noise_ref[:, cols] * tile
                if part == 0:
                    hit = base + ct * lanes == spot_at
                    value = value + jnp.where(hit, point_size, 0.0)
                lo_ref[b, part, :, cols] = value[:half]
                hi_ref[b, part, :, cols] = value[half:]


def sweep_kernel(depth, meta_ref, lo_ref, hi_ref, below_ref, above_ref, wave_ref, wbelow_ref,
                 wabove_ref, out_ref, are_ref, aim_ref, bre_ref, bim_ref, sre_ref, sim_ref, w_ref,
                 sr_ref, si_ref):
    half = depth // 2
    rows, cells = sre_ref.shape
    width = LANES
    chunks = cells // width
    slab = meta_ref[0]
    nslab = meta_ref[1]
    w_ref[0:HALO] = wbelow_ref[...]
    w_ref[HALO : HALO + depth] = wave_ref[...]
    w_ref[HALO + depth :] = wabove_ref[...]
    for part, dst in ((0, sre_ref), (1, sim_ref)):
        dst[0:HALO] = below_ref[0, part]
        dst[HALO : HALO + half] = lo_ref[0, part]
        dst[HALO + half : HALO + depth] = hi_ref[0, part]
        dst[HALO + depth :] = above_ref[0, part]
    zeros = jnp.zeros((rows, PAD), jnp.float32)
    for ref in (are_ref, aim_ref, bre_ref, bim_ref):
        ref[:, 0:PAD] = zeros
        ref[:, PAD + cells :] = zeros
    row = lax.broadcasted_iota(jnp.int32, (rows, width), 0)
    inside = jnp.logical_and(
        jnp.logical_or(row >= HALO, slab > 0),
        jnp.logical_or(row < HALO + depth, slab < nslab - 1),
    )

    def first(j, carry):
        c0 = pl.multiple_of(j * width, width)
        cols = pl.ds(c0, width)
        wave = w_ref[:, cols]
        diag_real = 6.0 - wave
        denom = diag_real * diag_real + damping * wave * (damping * wave)
        sr = jnp.where(inside, relaxation * diag_real / denom, 0.0)
        si = jnp.where(inside, relaxation * damping * wave / denom, 0.0)
        sr_ref[:, cols] = sr
        si_ref[:, cols] = si
        src_re = sre_ref[:, cols]
        src_im = sim_ref[:, cols]
        out = pl.ds(PAD + c0, width)
        are_ref[:, out] = sr * src_re - si * src_im
        aim_ref[:, out] = sr * src_im + si * src_re
        return carry

    lax.fori_loop(0, chunks, first, 0, unroll=True)

    keep = 1.0 - relaxation
    lane = lax.broadcasted_iota(jnp.int32, (rows, width), 1)
    col = jnp.bitwise_and(lane, GY - 1)
    has_ym = col != 0
    has_yp = col != GY - 1

    def sweep(src_pair, dst_pair, last):
        def chunk(j, carry):
            c0 = pl.multiple_of(j * width, width)
            cols = pl.ds(c0, width)

            def total(ref, src):
                ext = ref[:, pl.ds(c0, width + 2 * PAD)]
                rot = pltpu.roll(ext, GY, 1)
                mid = ext[:, PAD : PAD + width]
                xm = rot[:, PAD : PAD + width]
                xp = rot[:, 2 * PAD : 2 * PAD + width]
                ym = jnp.where(has_ym, pltpu.roll(mid, 1, 1), 0.0)
                yp = jnp.where(has_yp, pltpu.roll(mid, width - 1, 1), 0.0)
                dn = pltpu.roll(mid, 1, 0)
                up = pltpu.roll(mid, rows - 1, 0)
                return mid, src + (xm + xp + ym + yp + dn + up)

            re, t_re = total(src_pair[0], sre_ref[:, cols])
            im, t_im = total(src_pair[1], sim_ref[:, cols])
            s_r = sr_ref[:, cols]
            s_i = si_ref[:, cols]
            new_re = keep * re + (s_r * t_re - s_i * t_im)
            new_im = keep * im + (s_r * t_im + s_i * t_re)
            if last:
                out_ref[0, 0, :, cols] = new_re[HALO : HALO + depth]
                out_ref[1, 0, :, cols] = new_im[HALO : HALO + depth]
            else:
                dst_pair[0][:, pl.ds(PAD + c0, width)] = new_re
                dst_pair[1][:, pl.ds(PAD + c0, width)] = new_im
            return carry

        lax.fori_loop(0, chunks, chunk, 0, unroll=True)

    pairs = ((are_ref, aim_ref), (bre_ref, bim_ref))
    for k in range(SWEEPS - 1):
        sweep(pairs[k % 2], pairs[(k + 1) % 2], k == SWEEPS - 2)


def sweeps(meta, lo, hi, below, above, wave, wbelow, wabove):
    owned, _, half, cells = lo.shape
    depth = 2 * half
    rows = depth + 2 * HALO
    piece = pl.BlockSpec((1, 2, half, cells), lambda b, *_: (b, 0, 0, 0))
    halo = pl.BlockSpec((1, 2, HALO, cells), lambda b, *_: (b, 0, 0, 0))
    whole = lambda shape: pl.BlockSpec(shape, lambda b, *_: (0,) * len(shape))
    grid_spec = pltpu.PrefetchScalarGridSpec(
        num_scalar_prefetch=1,
        grid=(owned,),
        in_specs=[piece, piece, halo, halo, whole((depth, cells)), whole((HALO, cells)),
                  whole((HALO, cells))],
        out_specs=pl.BlockSpec((2, 1, depth, cells), lambda b, *_: (0, b, 0, 0)),
        scratch_shapes=[pltpu.VMEM((rows, cells + 2 * PAD), jnp.float32) for _ in range(4)]
        + [pltpu.VMEM((rows, cells), jnp.float32) for _ in range(5)],
    )
    return pl.pallas_call(
        functools.partial(sweep_kernel, depth),
        out_shape=jax.ShapeDtypeStruct((2, owned, depth, cells), jnp.float32),
        grid_spec=grid_spec,
        cost_estimate=pl.CostEstimate(
            flops=owned * SWEEPS * 60 * rows * cells,
            bytes_accessed=owned * 4 * cells * (6 * depth),
            transcendentals=0,
        ),
    )(meta, lo, hi, below, above, wave, wbelow, wabove)


def local(green_fields, pair_list, pair_values, noise_map, wave_square, station_cell):
    parts, owned, depth, cells = green_fields.shape
    nsta = lax.axis_size("sta")
    nslab = lax.axis_size("slab")
    count = owned * nsta
    lanes = cells // nsta
    slab = lax.axis_index("slab")
    up_pairs = [(i, i + 1) for i in range(nslab - 1)]
    down_pairs = [(i + 1, i) for i in range(nslab - 1)]
    half = depth // 2

    send = pl.pallas_call(
        pack_kernel,
        out_shape=jax.ShapeDtypeStruct((nsta, parts * owned * depth, lanes), green_fields.dtype),
    )(green_fields)
    recv = lax.all_to_all(send, "sta", 0, 0, tiled=True)

    big = build_resid(pair_list, pair_values, count)
    size = 2 * count
    new = jnp.arange(size, dtype=jnp.int32)
    old_row = (new % 2) * count + new // 2
    src, rest = new // (2 * owned), new % (2 * owned)
    old_col = (rest // owned) * count + src * owned + rest % owned
    pick_rows = (old_row[:, None] == new[None, :]).astype(jnp.bfloat16)
    pick_cols = (new[:, None] == old_col[None, :]).astype(jnp.bfloat16)
    big = jnp.dot(pick_rows, big, preferred_element_type=jnp.float32).astype(jnp.bfloat16)
    big = jnp.dot(big, pick_cols, preferred_element_type=jnp.float32).astype(jnp.bfloat16)
    big, wave_hi, wave_lo = lax.optimization_barrier(
        (big, wave_square[depth - HALO :], wave_square[:HALO])
    )
    wbelow = lax.ppermute(wave_hi, "slab", up_pairs)
    wabove = lax.ppermute(wave_lo, "slab", down_pairs)
    mixed = mix(big, recv.reshape(nsta * parts * owned * depth, lanes), depth)
    back = lax.all_to_all(mixed.reshape(nsta, owned * parts * depth, lanes), "sta", 0, 0,
                          tiled=True)
    back, wbelow, wabove = lax.optimization_barrier((back, wbelow, wabove))

    meta = jnp.concatenate(
        [jnp.stack([slab, jnp.int32(nslab)]).astype(jnp.int32), station_cell.astype(jnp.int32)]
    )
    lo, hi = pl.pallas_call(
        functools.partial(source_kernel, owned, depth),
        out_shape=[jax.ShapeDtypeStruct((owned, 2, half, cells), jnp.float32)] * 2,
        in_specs=[
            pl.BlockSpec(memory_space=pltpu.SMEM),
            pl.BlockSpec(memory_space=pltpu.VMEM),
            pl.BlockSpec(memory_space=pltpu.VMEM),
        ],
    )(meta, back, noise_map)
    below = lax.ppermute(hi, "slab", up_pairs)
    above = lax.ppermute(lo, "slab", down_pairs)
    return sweeps(meta, lo, hi, below, above, wave_square, wbelow, wabove)


def solution(mesh):
    placed = (P(None, "sta", "slab", None), P(), P(), P("slab", None), P("slab", None), P("sta"))
    return jax.shard_map(
        local, mesh=mesh, in_specs=placed, out_specs=P(None, "sta", "slab", None), check_vma=False
    )
```

```python
import functools

import jax
import jax.numpy as jnp
from jax import lax
from jax.experimental import pallas as pl
from jax.experimental.pallas import tpu as pltpu
from jax.sharding import PartitionSpec as P

GY = 64
SWEEPS = 6
HALO = 8
REACH = SWEEPS - 1
LANES = 512
PAD = 128

damping = 0.3
relaxation = 0.8
point_size = 2.0


def build_resid(pair_list, pair_values, count):
    labels = jnp.arange(count, dtype=jnp.int32)
    first = (pair_list[:, 0:1] == labels[None, :]).astype(jnp.float32)
    second = (pair_list[:, 1:2] == labels[None, :]).astype(jnp.float32)
    real_w = pair_values[0][:, None]
    imag_w = pair_values[1][:, None]
    highest = lax.Precision.HIGHEST
    resid_real = jnp.dot(
        first.T, real_w * second, precision=highest, preferred_element_type=jnp.float32
    ) + jnp.dot(second.T, real_w * first, precision=highest, preferred_element_type=jnp.float32)
    resid_imag = jnp.dot(
        first.T, imag_w * second, precision=highest, preferred_element_type=jnp.float32
    ) - jnp.dot(second.T, imag_w * first, precision=highest, preferred_element_type=jnp.float32)
    resid_real = resid_real.astype(jnp.bfloat16)
    resid_imag = resid_imag.astype(jnp.bfloat16)
    upper = jnp.concatenate([resid_real, -resid_imag], axis=1)
    lower = jnp.concatenate([resid_imag, resid_real], axis=1)
    return jnp.concatenate([upper, lower], axis=0)


def pack_kernel(green_ref, send_ref):
    parts, owned, depth, cells = green_ref.shape
    pieces, _, lanes = send_ref.shape
    for part in range(parts):
        for b in range(owned):
            start = (part * owned + b) * depth
            for ct in range(pieces):
                send_ref[ct, start : start + depth, :] = green_ref[part, b, :, ct * lanes : (ct + 1) * lanes]


def mix_kernel(depth, big_ref, recv_ref, out_ref, wide_ref, acc_ref):
    wide_ref[...] = recv_ref[...].astype(jnp.float32)
    big = big_ref[...]
    rows = big.shape[0]
    for r in range(depth):
        rhs = wide_ref[pl.ds(r, rows, stride=depth), :].astype(jnp.bfloat16)
        acc_ref[pl.ds(r, rows, stride=depth), :] = jnp.dot(
            big, rhs, preferred_element_type=jnp.float32
        )
    out_ref[...] = acc_ref[...].astype(out_ref.dtype)


def mix(big, recv, depth):
    total, lanes = recv.shape
    return pl.pallas_call(
        functools.partial(mix_kernel, depth),
        out_shape=jax.ShapeDtypeStruct((total, lanes), jnp.bfloat16),
        scratch_shapes=[
            pltpu.VMEM((total, lanes), jnp.float32),
            pltpu.VMEM((total, lanes), jnp.float32),
        ],
        cost_estimate=pl.CostEstimate(
            flops=2 * big.shape[0] * big.shape[1] * depth * lanes,
            bytes_accessed=4 * total * lanes,
            transcendentals=0,
        ),
    )(big, recv)


def source_kernel(owned, depth, meta_ref, recv_ref, noise_ref, lo_ref, hi_ref, dn_ref, up_ref):
    pieces, _, lanes = recv_ref.shape
    half = depth // 2
    slab = meta_ref[0]
    row = lax.broadcasted_iota(jnp.int32, (depth, lanes), 0)
    lane = lax.broadcasted_iota(jnp.int32, (depth, lanes), 1)
    base = (slab * depth + row) * (pieces * lanes) + lane
    for b in range(owned):
        spot_at = meta_ref[2 + b]
        for part in range(2):
            start = (b * 2 + part) * depth
            for ct in range(pieces):
                cols = slice(ct * lanes, (ct + 1) * lanes)
                tile = recv_ref[ct, start : start + depth, :].astype(jnp.float32)
                value = noise_ref[:, cols] * tile
                if part == 0:
                    hit = base + ct * lanes == spot_at
                    value = value + jnp.where(hit, point_size, 0.0)
                lo_ref[b, part, :, cols] = value[:half]
                hi_ref[b, part, :, cols] = value[half:]
                at = (b * 2 + part) * REACH
                dn_ref[at : at + REACH, cols] = value[:REACH]
                up_ref[at : at + REACH, cols] = value[depth - REACH :]


def sweep_kernel(depth, meta_ref, lo_ref, hi_ref, below_ref, above_ref, wave_ref, wbelow_ref,
                 wabove_ref, out_ref, are_ref, aim_ref, bre_ref, bim_ref, sre_ref, sim_ref, w_ref,
                 sr_ref, si_ref):
    half = depth // 2
    rows, cells = sre_ref.shape
    width = LANES
    chunks = cells // width
    slab = meta_ref[0]
    nslab = meta_ref[1]
    w_ref[0:HALO] = wbelow_ref[...]
    w_ref[HALO : HALO + depth] = wave_ref[...]
    w_ref[HALO + depth :] = wabove_ref[...]
    spare = jnp.zeros((HALO - REACH, cells), jnp.float32)
    for part, dst in ((0, sre_ref), (1, sim_ref)):
        dst[0 : HALO - REACH] = spare
        dst[HALO : HALO + half] = lo_ref[0, part]
        dst[HALO + half : HALO + depth] = hi_ref[0, part]
        dst[HALO + depth + REACH :] = spare
    owned = below_ref.shape[0] // (2 * REACH)
    for bb in range(owned):

        @pl.when(pl.program_id(0) == bb)
        def _():
            for part, dst in ((0, sre_ref), (1, sim_ref)):
                at = (bb * 2 + part) * REACH
                dst[HALO - REACH : HALO] = below_ref[at : at + REACH]
                dst[HALO + depth : HALO + depth + REACH] = above_ref[at : at + REACH]

    zeros = jnp.zeros((rows, PAD), jnp.float32)
    for ref in (are_ref, aim_ref, bre_ref, bim_ref):
        ref[:, 0:PAD] = zeros
        ref[:, PAD + cells :] = zeros
    row = lax.broadcasted_iota(jnp.int32, (rows, width), 0)
    inside = jnp.logical_and(
        jnp.logical_or(row >= HALO, slab > 0),
        jnp.logical_or(row < HALO + depth, slab < nslab - 1),
    )

    def first(j, carry):
        c0 = pl.multiple_of(j * width, width)
        cols = pl.ds(c0, width)
        wave = w_ref[:, cols]
        diag_real = 6.0 - wave
        denom = diag_real * diag_real + damping * wave * (damping * wave)
        sr = jnp.where(inside, relaxation * diag_real / denom, 0.0)
        si = jnp.where(inside, relaxation * damping * wave / denom, 0.0)
        sr_ref[:, cols] = sr
        si_ref[:, cols] = si
        src_re = sre_ref[:, cols]
        src_im = sim_ref[:, cols]
        out = pl.ds(PAD + c0, width)
        are_ref[:, out] = sr * src_re - si * src_im
        aim_ref[:, out] = sr * src_im + si * src_re
        return carry

    lax.fori_loop(0, chunks, first, 0, unroll=True)

    keep = 1.0 - relaxation
    lane = lax.broadcasted_iota(jnp.int32, (rows, width), 1)
    col = jnp.bitwise_and(lane, GY - 1)
    has_ym = col != 0
    has_yp = col != GY - 1

    def sweep(src_pair, dst_pair, last):
        def chunk(j, carry):
            c0 = pl.multiple_of(j * width, width)
            cols = pl.ds(c0, width)

            def total(ref, src):
                ext = ref[:, pl.ds(c0, width + 2 * PAD)]
                rot = pltpu.roll(ext, GY, 1)
                mid = ext[:, PAD : PAD + width]
                xm = rot[:, PAD : PAD + width]
                xp = rot[:, 2 * PAD : 2 * PAD + width]
                ym = jnp.where(has_ym, pltpu.roll(mid, 1, 1), 0.0)
                yp = jnp.where(has_yp, pltpu.roll(mid, width - 1, 1), 0.0)
                dn = pltpu.roll(mid, 1, 0)
                up = pltpu.roll(mid, rows - 1, 0)
                return mid, src + (xm + xp + ym + yp + dn + up)

            re, t_re = total(src_pair[0], sre_ref[:, cols])
            im, t_im = total(src_pair[1], sim_ref[:, cols])
            s_r = sr_ref[:, cols]
            s_i = si_ref[:, cols]
            new_re = keep * re + (s_r * t_re - s_i * t_im)
            new_im = keep * im + (s_r * t_im + s_i * t_re)
            if last:
                out_ref[0, 0, :, cols] = new_re[HALO : HALO + depth]
                out_ref[1, 0, :, cols] = new_im[HALO : HALO + depth]
            else:
                dst_pair[0][:, pl.ds(PAD + c0, width)] = new_re
                dst_pair[1][:, pl.ds(PAD + c0, width)] = new_im
            return carry

        lax.fori_loop(0, chunks, chunk, 0, unroll=True)

    pairs = ((are_ref, aim_ref), (bre_ref, bim_ref))
    for k in range(SWEEPS - 1):
        sweep(pairs[k % 2], pairs[(k + 1) % 2], k == SWEEPS - 2)


def sweeps(meta, lo, hi, below, above, wave, wbelow, wabove):
    owned, _, half, cells = lo.shape
    depth = 2 * half
    rows = depth + 2 * HALO
    piece = pl.BlockSpec((1, 2, half, cells), lambda b, *_: (b, 0, 0, 0))
    halo = pl.BlockSpec((owned * 2 * REACH, cells), lambda b, *_: (0, 0))
    whole = lambda shape: pl.BlockSpec(shape, lambda b, *_: (0,) * len(shape))
    grid_spec = pltpu.PrefetchScalarGridSpec(
        num_scalar_prefetch=1,
        grid=(owned,),
        in_specs=[piece, piece, halo, halo, whole((depth, cells)), whole((HALO, cells)),
                  whole((HALO, cells))],
        out_specs=pl.BlockSpec((2, 1, depth, cells), lambda b, *_: (0, b, 0, 0)),
        scratch_shapes=[pltpu.VMEM((rows, cells + 2 * PAD), jnp.float32) for _ in range(4)]
        + [pltpu.VMEM((rows, cells), jnp.float32) for _ in range(5)],
    )
    return pl.pallas_call(
        functools.partial(sweep_kernel, depth),
        out_shape=jax.ShapeDtypeStruct((2, owned, depth, cells), jnp.float32),
        grid_spec=grid_spec,
        cost_estimate=pl.CostEstimate(
            flops=owned * SWEEPS * 60 * rows * cells,
            bytes_accessed=owned * 4 * cells * (6 * depth),
            transcendentals=0,
        ),
    )(meta, lo, hi, below, above, wave, wbelow, wabove)


def local(green_fields, pair_list, pair_values, noise_map, wave_square, station_cell):
    parts, owned, depth, cells = green_fields.shape
    nsta = lax.axis_size("sta")
    nslab = lax.axis_size("slab")
    count = owned * nsta
    lanes = cells // nsta
    slab = lax.axis_index("slab")
    up_pairs = [(i, i + 1) for i in range(nslab - 1)]
    down_pairs = [(i + 1, i) for i in range(nslab - 1)]
    half = depth // 2

    send = pl.pallas_call(
        pack_kernel,
        out_shape=jax.ShapeDtypeStruct((nsta, parts * owned * depth, lanes), green_fields.dtype),
    )(green_fields)
    recv = lax.all_to_all(send, "sta", 0, 0, tiled=True)

    big = build_resid(pair_list, pair_values, count)
    size = 2 * count
    new = jnp.arange(size, dtype=jnp.int32)
    old_row = (new % 2) * count + new // 2
    src, rest = new // (2 * owned), new % (2 * owned)
    old_col = (rest // owned) * count + src * owned + rest % owned
    pick_rows = (old_row[:, None] == new[None, :]).astype(jnp.bfloat16)
    pick_cols = (new[:, None] == old_col[None, :]).astype(jnp.bfloat16)
    big = jnp.dot(pick_rows, big, preferred_element_type=jnp.float32).astype(jnp.bfloat16)
    big = jnp.dot(big, pick_cols, preferred_element_type=jnp.float32).astype(jnp.bfloat16)
    big, wave_hi, wave_lo = lax.optimization_barrier(
        (big, wave_square[depth - HALO :], wave_square[:HALO])
    )
    wbelow = lax.ppermute(wave_hi, "slab", up_pairs)
    wabove = lax.ppermute(wave_lo, "slab", down_pairs)
    mixed = mix(big, recv.reshape(nsta * parts * owned * depth, lanes), depth)
    back = lax.all_to_all(mixed.reshape(nsta, owned * parts * depth, lanes), "sta", 0, 0,
                          tiled=True)
    back, wbelow, wabove = lax.optimization_barrier((back, wbelow, wabove))

    meta = jnp.concatenate(
        [jnp.stack([slab, jnp.int32(nslab)]).astype(jnp.int32), station_cell.astype(jnp.int32)]
    )
    lo, hi, edge_dn, edge_up = pl.pallas_call(
        functools.partial(source_kernel, owned, depth),
        out_shape=[jax.ShapeDtypeStruct((owned, 2, half, cells), jnp.float32)] * 2
        + [jax.ShapeDtypeStruct((owned * 2 * REACH, cells), jnp.float32)] * 2,
        in_specs=[
            pl.BlockSpec(memory_space=pltpu.SMEM),
            pl.BlockSpec(memory_space=pltpu.VMEM),
            pl.BlockSpec(memory_space=pltpu.VMEM),
        ],
    )(meta, back, noise_map)
    below = lax.ppermute(edge_up, "slab", up_pairs)
    above = lax.ppermute(edge_dn, "slab", down_pairs)
    return sweeps(meta, lo, hi, below, above, wave_square, wbelow, wabove)


def solution(mesh):
    placed = (P(None, "sta", "slab", None), P(), P(), P("slab", None), P("slab", None), P("sta"))
    return jax.shard_map(
        local, mesh=mesh, in_specs=placed, out_specs=P(None, "sta", "slab", None), check_vma=False
    )
```

```python
import functools

import jax
import jax.numpy as jnp
from jax import lax
from jax.experimental import pallas as pl
from jax.experimental.pallas import tpu as pltpu
from jax.sharding import PartitionSpec as P

GY = 64
SWEEPS = 6
HALO = 8
LANES = 512
PAD = 128

damping = 0.3
relaxation = 0.8
point_size = 2.0


def build_resid(pair_list, pair_values, count):
    labels = jnp.arange(count, dtype=jnp.int32)
    first = (pair_list[:, 0:1] == labels[None, :]).astype(jnp.float32)
    second = (pair_list[:, 1:2] == labels[None, :]).astype(jnp.float32)
    real_w = pair_values[0][:, None]
    imag_w = pair_values[1][:, None]
    highest = lax.Precision.HIGHEST
    resid_real = jnp.dot(
        first.T, real_w * second, precision=highest, preferred_element_type=jnp.float32
    ) + jnp.dot(second.T, real_w * first, precision=highest, preferred_element_type=jnp.float32)
    resid_imag = jnp.dot(
        first.T, imag_w * second, precision=highest, preferred_element_type=jnp.float32
    ) - jnp.dot(second.T, imag_w * first, precision=highest, preferred_element_type=jnp.float32)
    resid_real = resid_real.astype(jnp.bfloat16)
    resid_imag = resid_imag.astype(jnp.bfloat16)
    upper = jnp.concatenate([resid_real, -resid_imag], axis=1)
    lower = jnp.concatenate([resid_imag, resid_real], axis=1)
    return jnp.concatenate([upper, lower], axis=0)


def pack_kernel(green_ref, send_ref):
    parts, owned, depth, cells = green_ref.shape
    pieces, _, lanes = send_ref.shape
    for part in range(parts):
        for b in range(owned):
            start = (part * owned + b) * depth
            for ct in range(pieces):
                send_ref[ct, start : start + depth, :] = green_ref[part, b, :, ct * lanes : (ct + 1) * lanes]


def mix_kernel(depth, big_ref, recv_ref, out_ref, acc_ref):
    big = big_ref[...]
    rows = big.shape[0]
    for r in range(depth):
        rhs = recv_ref[pl.ds(r, rows, stride=depth), :]
        acc_ref[pl.ds(r, rows, stride=depth), :] = jnp.dot(
            big, rhs, preferred_element_type=jnp.float32
        )
    out_ref[...] = acc_ref[...].astype(out_ref.dtype)


def mix(big, recv, depth):
    total, lanes = recv.shape
    return pl.pallas_call(
        functools.partial(mix_kernel, depth),
        out_shape=jax.ShapeDtypeStruct((total, lanes), jnp.bfloat16),
        scratch_shapes=[pltpu.VMEM((total, lanes), jnp.float32)],
        cost_estimate=pl.CostEstimate(
            flops=2 * big.shape[0] * big.shape[1] * depth * lanes,
            bytes_accessed=4 * total * lanes,
            transcendentals=0,
        ),
    )(big, recv)


def source_kernel(owned, depth, meta_ref, recv_ref, noise_ref, lo_ref, hi_ref):
    pieces, _, lanes = recv_ref.shape
    half = depth // 2
    slab = meta_ref[0]
    row = lax.broadcasted_iota(jnp.int32, (depth, lanes), 0)
    lane = lax.broadcasted_iota(jnp.int32, (depth, lanes), 1)
    base = (slab * depth + row) * (pieces * lanes) + lane
    for b in range(owned):
        spot_at = meta_ref[2 + b]
        for part in range(2):
            start = (b * 2 + part) * depth
            for ct in range(pieces):
                cols = slice(ct * lanes, (ct + 1) * lanes)
                tile = recv_ref[ct, start : start + depth, :].astype(jnp.float32)
                value = noise_ref[:, cols] * tile
                if part == 0:
                    hit = base + ct * lanes == spot_at
                    value = value + jnp.where(hit, point_size, 0.0)
                lo_ref[b, part, :, cols] = value[:half]
                hi_ref[b, part, :, cols] = value[half:]


def sweep_kernel(depth, meta_ref, lo_ref, hi_ref, below_ref, above_ref, wave_ref, wbelow_ref,
                 wabove_ref, out_ref, are_ref, aim_ref, bre_ref, bim_ref, sre_ref, sim_ref, w_ref,
                 sr_ref, si_ref):
    half = depth // 2
    rows, cells = sre_ref.shape
    width = LANES
    chunks = cells // width
    slab = meta_ref[0]
    nslab = meta_ref[1]
    w_ref[0:HALO] = wbelow_ref[...]
    w_ref[HALO : HALO + depth] = wave_ref[...]
    w_ref[HALO + depth :] = wabove_ref[...]
    for part, dst in ((0, sre_ref), (1, sim_ref)):
        dst[0:HALO] = below_ref[0, part]
        dst[HALO : HALO + half] = lo_ref[0, part]
        dst[HALO + half : HALO + depth] = hi_ref[0, part]
        dst[HALO + depth :] = above_ref[0, part]
    zeros = jnp.zeros((rows, PAD), jnp.float32)
    for ref in (are_ref, aim_ref, bre_ref, bim_ref):
        ref[:, 0:PAD] = zeros
        ref[:, PAD + cells :] = zeros
    row = lax.broadcasted_iota(jnp.int32, (rows, width), 0)
    inside = jnp.logical_and(
        jnp.logical_or(row >= HALO, slab > 0),
        jnp.logical_or(row < HALO + depth, slab < nslab - 1),
    )

    def first(j, carry):
        c0 = pl.multiple_of(j * width, width)
        cols = pl.ds(c0, width)
        wave = w_ref[:, cols]
        diag_real = 6.0 - wave
        denom = diag_real * diag_real + damping * wave * (damping * wave)
        sr = jnp.where(inside, relaxation * diag_real / denom, 0.0)
        si = jnp.where(inside, relaxation * damping * wave / denom, 0.0)
        sr_ref[:, cols] = sr
        si_ref[:, cols] = si
        src_re = sre_ref[:, cols]
        src_im = sim_ref[:, cols]
        out = pl.ds(PAD + c0, width)
        are_ref[:, out] = sr * src_re - si * src_im
        aim_ref[:, out] = sr * src_im + si * src_re
        return carry

    lax.fori_loop(0, chunks, first, 0, unroll=True)

    keep = 1.0 - relaxation
    lane = lax.broadcasted_iota(jnp.int32, (rows, width), 1)
    col = jnp.bitwise_and(lane, GY - 1)
    has_ym = col != 0
    has_yp = col != GY - 1

    def sweep(src_pair, dst_pair, last):
        def chunk(j, carry):
            c0 = pl.multiple_of(j * width, width)
            cols = pl.ds(c0, width)

            def total(ref, src):
                ext = ref[:, pl.ds(c0, width + 2 * PAD)]
                rot = pltpu.roll(ext, GY, 1)
                mid = ext[:, PAD : PAD + width]
                xm = rot[:, PAD : PAD + width]
                xp = rot[:, 2 * PAD : 2 * PAD + width]
                ym = jnp.where(has_ym, pltpu.roll(mid, 1, 1), 0.0)
                yp = jnp.where(has_yp, pltpu.roll(mid, width - 1, 1), 0.0)
                dn = pltpu.roll(mid, 1, 0)
                up = pltpu.roll(mid, rows - 1, 0)
                return mid, src + (xm + xp + ym + yp + dn + up)

            re, t_re = total(src_pair[0], sre_ref[:, cols])
            im, t_im = total(src_pair[1], sim_ref[:, cols])
            s_r = sr_ref[:, cols]
            s_i = si_ref[:, cols]
            new_re = keep * re + (s_r * t_re - s_i * t_im)
            new_im = keep * im + (s_r * t_im + s_i * t_re)
            if last:
                out_ref[0, 0, :, cols] = new_re[HALO : HALO + depth]
                out_ref[1, 0, :, cols] = new_im[HALO : HALO + depth]
            else:
                dst_pair[0][:, pl.ds(PAD + c0, width)] = new_re
                dst_pair[1][:, pl.ds(PAD + c0, width)] = new_im
            return carry

        lax.fori_loop(0, chunks, chunk, 0, unroll=True)

    pairs = ((are_ref, aim_ref), (bre_ref, bim_ref))
    for k in range(SWEEPS - 1):
        sweep(pairs[k % 2], pairs[(k + 1) % 2], k == SWEEPS - 2)


def sweeps(meta, lo, hi, below, above, wave, wbelow, wabove):
    owned, _, half, cells = lo.shape
    depth = 2 * half
    rows = depth + 2 * HALO
    piece = pl.BlockSpec((1, 2, half, cells), lambda b, *_: (b, 0, 0, 0))
    halo = pl.BlockSpec((1, 2, HALO, cells), lambda b, *_: (b, 0, 0, 0))
    whole = lambda shape: pl.BlockSpec(shape, lambda b, *_: (0,) * len(shape))
    grid_spec = pltpu.PrefetchScalarGridSpec(
        num_scalar_prefetch=1,
        grid=(owned,),
        in_specs=[piece, piece, halo, halo, whole((depth, cells)), whole((HALO, cells)),
                  whole((HALO, cells))],
        out_specs=pl.BlockSpec((2, 1, depth, cells), lambda b, *_: (0, b, 0, 0)),
        scratch_shapes=[pltpu.VMEM((rows, cells + 2 * PAD), jnp.float32) for _ in range(4)]
        + [pltpu.VMEM((rows, cells), jnp.float32) for _ in range(5)],
    )
    return pl.pallas_call(
        functools.partial(sweep_kernel, depth),
        out_shape=jax.ShapeDtypeStruct((2, owned, depth, cells), jnp.float32),
        grid_spec=grid_spec,
        cost_estimate=pl.CostEstimate(
            flops=owned * SWEEPS * 60 * rows * cells,
            bytes_accessed=owned * 4 * cells * (6 * depth),
            transcendentals=0,
        ),
    )(meta, lo, hi, below, above, wave, wbelow, wabove)


def local(green_fields, pair_list, pair_values, noise_map, wave_square, station_cell):
    parts, owned, depth, cells = green_fields.shape
    nsta = lax.axis_size("sta")
    nslab = lax.axis_size("slab")
    count = owned * nsta
    lanes = cells // nsta
    slab = lax.axis_index("slab")
    up_pairs = [(i, i + 1) for i in range(nslab - 1)]
    down_pairs = [(i + 1, i) for i in range(nslab - 1)]
    half = depth // 2

    send = pl.pallas_call(
        pack_kernel,
        out_shape=jax.ShapeDtypeStruct((nsta, parts * owned * depth, lanes), green_fields.dtype),
    )(green_fields)
    recv = lax.all_to_all(send, "sta", 0, 0, tiled=True)

    big = build_resid(pair_list, pair_values, count)
    size = 2 * count
    new = jnp.arange(size, dtype=jnp.int32)
    old_row = (new % 2) * count + new // 2
    src, rest = new // (2 * owned), new % (2 * owned)
    old_col = (rest // owned) * count + src * owned + rest % owned
    pick_rows = (old_row[:, None] == new[None, :]).astype(jnp.bfloat16)
    pick_cols = (new[:, None] == old_col[None, :]).astype(jnp.bfloat16)
    big = jnp.dot(pick_rows, big, preferred_element_type=jnp.float32).astype(jnp.bfloat16)
    big = jnp.dot(big, pick_cols, preferred_element_type=jnp.float32).astype(jnp.bfloat16)
    big, wave_hi, wave_lo = lax.optimization_barrier(
        (big, wave_square[depth - HALO :], wave_square[:HALO])
    )
    wbelow = lax.ppermute(wave_hi, "slab", up_pairs)
    wabove = lax.ppermute(wave_lo, "slab", down_pairs)
    mixed = mix(big, recv.reshape(nsta * parts * owned * depth, lanes), depth)
    back = lax.all_to_all(mixed.reshape(nsta, owned * parts * depth, lanes), "sta", 0, 0,
                          tiled=True)
    back, wbelow, wabove = lax.optimization_barrier((back, wbelow, wabove))

    meta = jnp.concatenate(
        [jnp.stack([slab, jnp.int32(nslab)]).astype(jnp.int32), station_cell.astype(jnp.int32)]
    )
    lo, hi = pl.pallas_call(
        functools.partial(source_kernel, owned, depth),
        out_shape=[jax.ShapeDtypeStruct((owned, 2, half, cells), jnp.float32)] * 2,
        in_specs=[
            pl.BlockSpec(memory_space=pltpu.SMEM),
            pl.BlockSpec(memory_space=pltpu.VMEM),
            pl.BlockSpec(memory_space=pltpu.VMEM),
        ],
    )(meta, back, noise_map)
    below = lax.ppermute(hi, "slab", up_pairs)
    above = lax.ppermute(lo, "slab", down_pairs)
    return sweeps(meta, lo, hi, below, above, wave_square, wbelow, wabove)


def solution(mesh):
    placed = (P(None, "sta", "slab", None), P(), P(), P("slab", None), P("slab", None), P("sta"))
    return jax.shard_map(
        local, mesh=mesh, in_specs=placed, out_specs=P(None, "sta", "slab", None), check_vma=False
    )
```
